32 devices in a mesh: dom: 8 (over z, core), loop: 4 (over y, x).
Axes of the slice: x: 2, y: 2, z: 4, core: 2. Of those that a mesh axis runs over, the one named last changes fastest.
Arguments:
- cotangent: bfloat16 [32768, 256], P(('dom', 'loop')), may hold values from -6 to 6
- preact: bfloat16 [32768, 256], P(('dom', 'loop')), may hold values from -6 to 6
- aggregated: bfloat16 [32768, 256], P(('dom', 'loop')), may hold values from -6 to 6
- weight: bfloat16 [256, 256], replicated, may hold values from -0.375 to 0.375
- tile_values: bfloat16 [20480, 128, 128], P(('dom', 'loop')), as said below
- tile_rows: int32 [32, 640], P(('dom', 'loop')), may hold values from 0 to 31
- tile_cols: int32 [32, 640], P(('dom', 'loop')), may hold values from 0 to 63, as said below
- tile_counts: int32 [32], P(('dom', 'loop')), may hold values from 32 to 640
Outputs:
- node_grad: float32 [32768, 256], P(('dom', 'loop'))
- weight_grad: float32 [256, 256], replicated
The draws below stay inside these ranges and needn't reach their ends.
Inputs may be any that keep to these rules, and one draw needn't show every extreme that they name: `tile_cols`: the live tiles of one device touch, for every dom index, exactly 4 distinct column blocks, and every tile's column lies among them. `tile_values`: entries are nonnegative.
All inputs are finite; a program needn't handle non-finite values.
Results may differ from the reference program's by a relative error of at most 0.0029.
Values may be sent and summed in bfloat16 or wider, within the bound.
No kernel may reach another device: no remote copies, remote signals or barrier semaphores. Data moves between devices by JAX's collectives and lax.ppermute only.
A program may use at most 192 MiB of HBM per device.

```python
import math
import jax
import jax.numpy as jnp
from jax import lax

F = 256
TILE = 128
RB_DEV = 8
CAP = 4
TILES_DEV = 640
NODES = 32768
N_DOM = 8
N_LOOP = 4
DEVICES = 32


def draw_tile_values(key, part):
    scale = (TILE * TILES_DEV // RB_DEV) ** (-0.5)
    shape = (DEVICES * TILES_DEV, TILE, TILE)
    values = jnp.minimum(jnp.abs(jax.random.normal(jax.random.fold_in(key, 32), shape, jnp.float32)), 6.0) * scale
    return values.astype(jnp.bfloat16)


def draw_tile_cols(key, part):
    keys = jax.random.split(jax.random.fold_in(key, 11), DEVICES * N_DOM)
    orders = jax.vmap(lambda single: jax.random.permutation(single, RB_DEV))(keys).reshape(DEVICES, N_DOM, RB_DEV)
    chosen = orders[:, :, :CAP]
    allowed = (jnp.arange(N_DOM, dtype=jnp.int32)[None, :, None] * RB_DEV + chosen).reshape(DEVICES, N_DOM * CAP)
    keys_two = jax.random.split(jax.random.fold_in(key, 12), DEVICES)
    spread = jax.vmap(lambda single: jax.random.permutation(single, N_DOM * CAP))(keys_two)
    first = jnp.take_along_axis(allowed, spread, axis=1)
    extra = jax.random.randint(jax.random.fold_in(key, 13), (DEVICES, TILES_DEV - N_DOM * CAP), 0, N_DOM * CAP)
    second = jnp.take_along_axis(allowed, extra, axis=1)
    return jnp.concatenate([first, second], axis=1).astype(jnp.int32)


def draw_tile_counts(key, part):
    lowest = N_DOM * CAP
    span = TILES_DEV - lowest
    first = jax.random.randint(jax.random.fold_in(key, 21), (DEVICES,), 0, span + 1)
    second = jax.random.randint(jax.random.fold_in(key, 22), (DEVICES,), 0, span + 1)
    counts = lowest + first * second // max(span, 1)
    fullest = jax.random.randint(jax.random.fold_in(key, 23), (), 0, DEVICES)
    return counts.at[fullest].set(TILES_DEV).astype(jnp.int32)


def with_ends(array, key, least, largest):
    place = [jax.random.randint(jax.random.fold_in(key, axis), (), 0, length) for axis, length in enumerate(array.shape)]
    longest = array.shape.index(max(array.shape))
    beside = place[:longest] + [(place[longest] + 1) % array.shape[longest]] + place[longest + 1:]
    return array.at[tuple(place)].set(least).at[tuple(beside)].set(largest)


def levels(key, dims, cuts, smallest, largest):
    gain = 1.0
    for position, parts in cuts:
        steps = jax.random.uniform(jax.random.fold_in(jax.random.fold_in(key, 6), position), (parts,), jnp.float32, smallest / len(cuts), largest / len(cuts))
        gain = gain * jnp.repeat(jnp.exp(steps), dims[position] // parts).reshape((-1,) + (1,) * (len(dims) - 1 - position))
    return gain


def gaussian(stream_key, extent, scale, limit, cuts=(), held_as=jnp.bfloat16):
    entries = scale * jax.random.normal(stream_key, extent, jnp.float32)
    if cuts:
        entries = entries * levels(stream_key, extent, cuts, -0.22, 0.18)
    return jnp.clip(entries, -limit, limit).astype(held_as)


def setup_inputs(seed: int = 0) -> dict:
    key_list = jax.random.split(jax.random.key(seed), 9)
    return {
        "cotangent": gaussian(key_list[0], (NODES, F), 1.0, 6.0, ((0, 32),)),
        "preact": gaussian(key_list[1], (NODES, F), 1.0, 6.0, ((0, 32),)),
        "aggregated": gaussian(key_list[2], (NODES, F), 1.0, 6.0, ((0, 32),)),
        "weight": gaussian(key_list[3], (F, F), F ** -0.5, 0.375),
        "tile_values": draw_tile_values(jax.random.fold_in(key_list[8], 71), 0),
        "tile_rows": with_ends(jax.random.randint(key_list[5], (DEVICES, TILES_DEV), 0, N_LOOP * RB_DEV), jax.random.fold_in(key_list[5], 1), 0, (N_LOOP * RB_DEV) - 1).astype(jnp.int32),
        "tile_cols": draw_tile_cols(jax.random.fold_in(key_list[8], 71), 0),
        "tile_counts": draw_tile_counts(jax.random.fold_in(key_list[8], 71), 0),
    }


def reference(cotangent, preact, aggregated, weight, tile_values, tile_rows, tile_cols, tile_counts):
    masked = jnp.where(preact > 0, cotangent, jnp.zeros_like(cotangent))
    weight_grad = jnp.dot(aggregated.T, masked, preferred_element_type=jnp.float32) * (1.0 / math.sqrt(NODES))
    projected = jnp.dot(masked, weight.T, preferred_element_type=jnp.float32).astype(jnp.bfloat16)
    row_blocks = projected.reshape(NODES // TILE, TILE, F)
    part_blocks = N_LOOP * RB_DEV
    values = tile_values.reshape(DEVICES, TILES_DEV, TILE, TILE)

    def one_device(totals, item):
        index, tile_vals, rows_here, cols_here, count = item
        dom_index = index // N_LOOP
        loop_index = index % N_LOOP
        source = (dom_index * part_blocks + rows_here).astype(jnp.int32)
        target = (cols_here // RB_DEV * part_blocks + loop_index * RB_DEV + cols_here % RB_DEV).astype(jnp.int32)
        picked = row_blocks[source].astype(jnp.float32)
        terms = jnp.einsum('tij,tif->tjf', tile_vals.astype(jnp.float32), picked, precision=lax.Precision.HIGHEST)
        alive = (jnp.arange(TILES_DEV, dtype=jnp.int32) < count).astype(jnp.float32)
        return (totals.at[target].add(terms * alive[:, None, None]), None)
    start = jnp.zeros((NODES // TILE, TILE, F), jnp.float32)
    totals = lax.scan(one_device, start, (jnp.arange(DEVICES, dtype=jnp.int32), values, tile_rows, tile_cols, tile_counts))[0]
    return (totals.reshape(NODES, F), weight_grad)
```

```python
import math

import jax
import jax.numpy as jnp
from jax import lax
from jax.experimental import pallas as pl
from jax.experimental.pallas import tpu as pltpu
from jax.sharding import PartitionSpec as P

GROUP = 32


def _spmm_kernel(rows_ref, cols_ref, cnt_ref, tv_ref, part_ref, out_ref):
    g = pl.program_id(0)
    count = cnt_ref[0]
    group = tv_ref.shape[0]
    base = g * group

    @pl.when(g == 0)
    def _():
        out_ref[...] = jnp.zeros(out_ref.shape, out_ref.dtype)

    @pl.when(base < count)
    def _():
        def body(t, carry):
            j = base + t

            @pl.when(j < count)
            def _():
                r = rows_ref[j]
                c = cols_ref[j]
                term = lax.dot_general(
                    tv_ref[t],
                    part_ref[r],
                    (((0,), (0,)), ((), ())),
                    preferred_element_type=jnp.float32,
                )
                out_ref[c] += term

            return carry

        lax.fori_loop(0, group, body, 0)


def _spmm(rows, cols, count, tile_values, partition, out_blocks):
    tiles, tile_size, _ = tile_values.shape
    part_blocks, _, width = partition.shape
    group = math.gcd(tiles, GROUP)

    def tv_map(g, rows_ref, cols_ref, cnt_ref):
        last = jnp.maximum((cnt_ref[0] + group - 1) // group - 1, 0)
        return (jnp.minimum(g, last), 0, 0)

    def whole(g, rows_ref, cols_ref, cnt_ref):
        return (0, 0, 0)

    return pl.pallas_call(
        _spmm_kernel,
        out_shape=jax.ShapeDtypeStruct((out_blocks, tile_size, width), jnp.float32),
        grid_spec=pltpu.PrefetchScalarGridSpec(
            num_scalar_prefetch=3,
            grid=(tiles // group,),
            in_specs=[
                pl.BlockSpec((group, tile_size, tile_size), tv_map),
                pl.BlockSpec((part_blocks, tile_size, width), whole),
            ],
            out_specs=pl.BlockSpec((out_blocks, tile_size, width), whole),
        ),
        compiler_params=pltpu.CompilerParams(
            dimension_semantics=("arbitrary",),
            vmem_limit_bytes=100 * 1024 * 1024 // 2,
        ),
    )(rows, cols, count, tile_values, partition)


def shards(cotangent, preact, aggregated, weight, tile_values, tile_rows, tile_cols, tile_counts):
    node_rows, width = cotangent.shape
    tile_size = tile_values.shape[1]
    dom_count = lax.axis_size("dom")
    total_nodes = node_rows * dom_count * lax.axis_size("loop")
    local_blocks = node_rows // tile_size
    all_blocks = dom_count * local_blocks
    masked = jnp.where(preact > 0, cotangent, jnp.zeros_like(cotangent))
    weight_term = jnp.dot(aggregated.T, masked, preferred_element_type=jnp.float32) * (
        1.0 / math.sqrt(total_nodes)
    )
    weight_grad = lax.psum(weight_term, ("dom", "loop"))
    projected = jnp.dot(masked, weight.T, preferred_element_type=jnp.float32).astype(jnp.bfloat16)
    partition = lax.all_gather(projected, "loop", axis=0, tiled=True)
    part_blocks = partition.shape[0] // tile_size
    partition = partition.reshape(part_blocks, tile_size, width)
    adjoint = _spmm(tile_rows[0], tile_cols[0], tile_counts, tile_values, partition, all_blocks)
    node_grad = lax.psum_scatter(
        adjoint.reshape(all_blocks * tile_size, width), "dom", scatter_dimension=0, tiled=True
    )
    return (node_grad, weight_grad)


def solution(mesh):
    return jax.shard_map(
        shards,
        mesh=mesh,
        in_specs=(
            P(("dom", "loop"), None),
            P(("dom", "loop"), None),
            P(("dom", "loop"), None),
            P(),
            P(("dom", "loop"), None, None),
            P(("dom", "loop"), None),
            P(("dom", "loop"), None),
            P(("dom", "loop")),
        ),
        out_specs=(P(("dom", "loop"), None), P()),
        check_vma=False,
    )
```

```python
import math

import jax
import jax.numpy as jnp
from jax import lax
from jax.experimental import pallas as pl
from jax.experimental.pallas import tpu as pltpu
from jax.sharding import PartitionSpec as P

GROUP = 32
CAP = 4


def _spmm_kernel(rows_ref, slots_ref, cnt_ref, tv_ref, part_ref, out_ref):
    g = pl.program_id(0)
    count = cnt_ref[0]
    group = tv_ref.shape[0]
    base = g * group

    @pl.when(g == 0)
    def _():
        out_ref[...] = jnp.zeros(out_ref.shape, out_ref.dtype)

    @pl.when(base < count)
    def _():
        def body(t, carry):
            j = base + t

            @pl.when(j < count)
            def _():
                r = rows_ref[j]
                c = slots_ref[j]
                term = lax.dot_general(
                    tv_ref[t],
                    part_ref[r],
                    (((0,), (0,)), ((), ())),
                    preferred_element_type=jnp.float32,
                )
                out_ref[c] += term

            return carry

        lax.fori_loop(0, group, body, 0)


def _spmm(rows, slots, count, tile_values, partition, out_blocks):
    tiles, tile_size, _ = tile_values.shape
    part_blocks, _, width = partition.shape
    group = math.gcd(tiles, GROUP)

    def tv_map(g, rows_ref, slots_ref, cnt_ref):
        last = jnp.maximum((cnt_ref[0] + group - 1) // group - 1, 0)
        return (jnp.minimum(g, last), 0, 0)

    def whole(g, rows_ref, slots_ref, cnt_ref):
        return (0, 0, 0)

    return pl.pallas_call(
        _spmm_kernel,
        out_shape=jax.ShapeDtypeStruct((out_blocks, tile_size, width), jnp.float32),
        grid_spec=pltpu.PrefetchScalarGridSpec(
            num_scalar_prefetch=3,
            grid=(tiles // group,),
            in_specs=[
                pl.BlockSpec((group, tile_size, tile_size), tv_map),
                pl.BlockSpec((part_blocks, tile_size, width), whole),
            ],
            out_specs=pl.BlockSpec((out_blocks, tile_size, width), whole),
        ),
        compiler_params=pltpu.CompilerParams(
            dimension_semantics=("arbitrary",),
            vmem_limit_bytes=50 * 1024 * 1024,
        ),
    )(rows, slots, count, tile_values, partition)


def _combine_kernel(map_ref, recv_ref, out_ref):
    g = pl.program_id(0)
    per = recv_ref.shape[0]

    @pl.when(g == 0)
    def _():
        out_ref[...] = jnp.zeros(out_ref.shape, out_ref.dtype)

    for k in range(per):
        b = map_ref[g * per + k]
        out_ref[b] += recv_ref[k]


def _combine(block_map, received, out_blocks):
    total, tile_size, width = received.shape
    per = CAP

    def recv_map(g, map_ref):
        return (g, 0, 0)

    def whole(g, map_ref):
        return (0, 0, 0)

    return pl.pallas_call(
        _combine_kernel,
        out_shape=jax.ShapeDtypeStruct((out_blocks, tile_size, width), jnp.float32),
        grid_spec=pltpu.PrefetchScalarGridSpec(
            num_scalar_prefetch=1,
            grid=(total // per,),
            in_specs=[pl.BlockSpec((per, tile_size, width), recv_map)],
            out_specs=pl.BlockSpec((out_blocks, tile_size, width), whole),
        ),
        compiler_params=pltpu.CompilerParams(dimension_semantics=("arbitrary",)),
    )(block_map, received)


def _tree_sum(x, axis):
    size = lax.axis_size(axis)
    if size & (size - 1):
        return lax.psum(x, axis)
    step = 1
    while step < size:
        pairs = [(i, i ^ step) for i in range(size)]
        x = x + lax.ppermute(x, axis, pairs)
        step *= 2
    return x


def shards(cotangent, preact, aggregated, weight, tile_values, tile_rows, tile_cols, tile_counts):
    node_rows, width = cotangent.shape
    tile_size = tile_values.shape[1]
    dom_count = lax.axis_size("dom")
    loop_count = lax.axis_size("loop")
    dom_index = lax.axis_index("dom")
    loop_index = lax.axis_index("loop")
    total_nodes = node_rows * dom_count * loop_count
    local_blocks = node_rows // tile_size
    tile_total = tile_rows.shape[1]

    masked = jnp.where(preact > 0, cotangent, jnp.zeros_like(cotangent))
    weight_term = jnp.dot(aggregated.T, masked, preferred_element_type=jnp.float32) * (
        1.0 / math.sqrt(total_nodes)
    )
    weight_grad = _tree_sum(_tree_sum(weight_term, "loop"), "dom")

    projected = jnp.dot(masked, weight.T, preferred_element_type=jnp.float32).astype(jnp.bfloat16)
    pieces = [projected]
    for shift in range(1, loop_count):
        pairs = [(i, (i + shift) % loop_count) for i in range(loop_count)]
        pieces.append(lax.ppermute(projected, "loop", pairs))
    partition = jnp.concatenate(pieces, axis=0).reshape(
        loop_count * local_blocks, tile_size, width
    )

    rows = tile_rows[0]
    source_loop = rows // local_blocks
    rows = ((loop_index - source_loop) % loop_count) * local_blocks + rows % local_blocks

    cols = tile_cols[0]
    live = jnp.arange(tile_total, dtype=jnp.int32) < tile_counts[0]
    all_blocks = dom_count * local_blocks
    hits = (cols[:, None] == jnp.arange(all_blocks, dtype=jnp.int32)[None, :]) & live[:, None]
    present = jnp.any(hits, axis=0).reshape(dom_count, local_blocks).astype(jnp.int32)
    rank = jnp.cumsum(present, axis=1) - 1
    block_ids = jnp.arange(local_blocks, dtype=jnp.int32)
    table = jnp.stack(
        [jnp.sum(jnp.where((rank == k) & (present > 0), block_ids[None, :], 0), axis=1) for k in range(CAP)],
        axis=1,
    )
    order = (jnp.arange(dom_count, dtype=jnp.int32) + dom_index) % dom_count
    table = table[order]
    dest_dom = cols // local_blocks
    tile_rank = jnp.clip(rank.reshape(-1)[cols], 0, CAP - 1)
    slots = ((dest_dom - dom_index) % dom_count) * CAP + tile_rank

    compact = _spmm(rows, slots, tile_counts, tile_values, partition, dom_count * CAP)

    received = [compact[:CAP]]
    maps = [table[0]]
    for shift in range(1, dom_count):
        pairs = [(i, (i + shift) % dom_count) for i in range(dom_count)]
        slab, ids = lax.ppermute(
            (compact[shift * CAP:(shift + 1) * CAP], table[shift]), "dom", pairs
        )
        received.append(slab)
        maps.append(ids)
    node_grad = _combine(
        jnp.concatenate(maps), jnp.concatenate(received, axis=0), local_blocks
    ).reshape(node_rows, width)
    return (node_grad, weight_grad)


def solution(mesh):
    return jax.shard_map(
        shards,
        mesh=mesh,
        in_specs=(
            P(("dom", "loop"), None),
            P(("dom", "loop"), None),
            P(("dom", "loop"), None),
            P(),
            P(("dom", "loop"), None, None),
            P(("dom", "loop"), None),
            P(("dom", "loop"), None),
            P(("dom", "loop")),
        ),
        out_specs=(P(("dom", "loop"), None), P()),
        check_vma=False,
    )
```

```python
import math

import jax
import jax.numpy as jnp
from jax import lax
from jax.experimental import pallas as pl
from jax.experimental.pallas import tpu as pltpu
from jax.sharding import PartitionSpec as P

GROUP = 32
CAP = 4


def _spmm_kernel(rows_ref, slots_ref, cnt_ref, tv_ref, part_ref, out_ref):
    g = pl.program_id(0)
    count = cnt_ref[0]
    group = tv_ref.shape[0]
    base = g * group

    @pl.when(g == 0)
    def _():
        out_ref[...] = jnp.zeros(out_ref.shape, out_ref.dtype)

    @pl.when(base < count)
    def _():
        for t in range(group):
            j = base + t
            r = rows_ref[j]
            c = slots_ref[j]
            term = lax.dot_general(
                tv_ref[t],
                part_ref[r],
                (((0,), (0,)), ((), ())),
                preferred_element_type=jnp.float32,
            )
            out_ref[c] += jnp.where(j < count, term, 0.0)


def _spmm(rows, slots, count, tile_values, partition, out_blocks):
    tiles, tile_size, _ = tile_values.shape
    part_blocks, _, width = partition.shape
    group = math.gcd(tiles, GROUP)

    def tv_map(g, rows_ref, slots_ref, cnt_ref):
        last = jnp.maximum((cnt_ref[0] + group - 1) // group - 1, 0)
        return (jnp.minimum(g, last), 0, 0)

    def whole(g, rows_ref, slots_ref, cnt_ref):
        return (0, 0, 0)

    return pl.pallas_call(
        _spmm_kernel,
        out_shape=jax.ShapeDtypeStruct((out_blocks, tile_size, width), jnp.float32),
        grid_spec=pltpu.PrefetchScalarGridSpec(
            num_scalar_prefetch=3,
            grid=(tiles // group,),
            in_specs=[
                pl.BlockSpec((group, tile_size, tile_size), tv_map),
                pl.BlockSpec((part_blocks, tile_size, width), whole),
            ],
            out_specs=pl.BlockSpec((out_blocks, tile_size, width), whole),
        ),
        compiler_params=pltpu.CompilerParams(
            dimension_semantics=("arbitrary",),
            vmem_limit_bytes=50 * 1024 * 1024,
        ),
    )(rows, slots, count, tile_values, partition)


def _combine_kernel(map_ref, recv_ref, out_ref):
    g = pl.program_id(0)
    per = recv_ref.shape[0]

    @pl.when(g == 0)
    def _():
        out_ref[...] = jnp.zeros(out_ref.shape, out_ref.dtype)

    for k in range(per):
        b = map_ref[g * per + k]
        out_ref[b] += recv_ref[k]


def _combine(block_map, received, out_blocks):
    total, tile_size, width = received.shape
    per = CAP

    def recv_map(g, map_ref):
        return (g, 0, 0)

    def whole(g, map_ref):
        return (0, 0, 0)

    return pl.pallas_call(
        _combine_kernel,
        out_shape=jax.ShapeDtypeStruct((out_blocks, tile_size, width), jnp.float32),
        grid_spec=pltpu.PrefetchScalarGridSpec(
            num_scalar_prefetch=1,
            grid=(total // per,),
            in_specs=[pl.BlockSpec((per, tile_size, width), recv_map)],
            out_specs=pl.BlockSpec((out_blocks, tile_size, width), whole),
        ),
        compiler_params=pltpu.CompilerParams(dimension_semantics=("arbitrary",)),
    )(block_map, received)


def _pick(stacked, index):
    return lax.dynamic_index_in_dim(stacked, index, axis=0, keepdims=False)


def shards(cotangent, preact, aggregated, weight, tile_values, tile_rows, tile_cols, tile_counts):
    node_rows, width = cotangent.shape
    tile_size = tile_values.shape[1]
    dom_count = lax.axis_size("dom")
    loop_count = lax.axis_size("loop")
    dom_index = lax.axis_index("dom")
    loop_index = lax.axis_index("loop")
    total_nodes = node_rows * dom_count * loop_count
    local_blocks = node_rows // tile_size
    tile_total = tile_rows.shape[1]

    masked = jnp.where(preact > 0, cotangent, jnp.zeros_like(cotangent))
    weight_term = jnp.dot(aggregated.T, masked, preferred_element_type=jnp.float32) * (
        1.0 / math.sqrt(total_nodes)
    )
    projected = jnp.dot(masked, weight.T, preferred_element_type=jnp.float32).astype(jnp.bfloat16)

    pieces = [projected]
    terms = [weight_term]
    for shift in range(1, loop_count):
        pairs = [(i, (i + shift) % loop_count) for i in range(loop_count)]
        piece, term = lax.ppermute((projected, weight_term), "loop", pairs)
        pieces.append(piece)
        terms.append(term)
    partition = jnp.concatenate(pieces, axis=0).reshape(
        loop_count * local_blocks, tile_size, width
    )
    terms = jnp.stack(terms)
    loop_sum = _pick(terms, loop_index % loop_count)
    for source in range(1, loop_count):
        loop_sum = loop_sum + _pick(terms, (loop_index - source) % loop_count)

    rows = tile_rows[0]
    source_loop = rows // local_blocks
    rows = ((loop_index - source_loop) % loop_count) * local_blocks + rows % local_blocks

    cols = tile_cols[0]
    live = jnp.arange(tile_total, dtype=jnp.int32) < tile_counts[0]
    all_blocks = dom_count * local_blocks
    onehot = cols[:, None] == jnp.arange(all_blocks, dtype=jnp.int32)[None, :]
    present = jnp.any(onehot & live[:, None], axis=0).reshape(dom_count, local_blocks)
    present = present.astype(jnp.int32)
    rank = jnp.cumsum(present, axis=1) - 1
    tile_rank = jnp.sum(jnp.where(onehot, rank.reshape(1, -1), 0), axis=1)
    tile_rank = jnp.clip(tile_rank, 0, CAP - 1)
    block_ids = jnp.arange(local_blocks, dtype=jnp.int32)
    table = jnp.stack(
        [jnp.sum(jnp.where((rank == k) & (present > 0), block_ids[None, :], 0), axis=1) for k in range(CAP)],
        axis=1,
    )
    dom_ids = jnp.arange(dom_count, dtype=jnp.int32)
    rotate = ((dom_ids[:, None] + dom_index) % dom_count) == dom_ids[None, :]
    table = jnp.sum(jnp.where(rotate[:, :, None], table[None, :, :], 0), axis=1)
    dest_dom = cols // local_blocks
    slots = ((dest_dom - dom_index) % dom_count) * CAP + tile_rank

    compact = _spmm(rows, slots, tile_counts, tile_values, partition, dom_count * CAP)

    chunk = width // dom_count
    chunks = loop_sum.reshape(dom_count, chunk, width)
    received = [compact[:CAP]]
    maps = [table[0]]
    parts = [_pick(chunks, dom_index)]
    for shift in range(1, dom_count):
        pairs = [(i, (i + shift) % dom_count) for i in range(dom_count)]
        slab, ids, part = lax.ppermute(
            (compact[shift * CAP:(shift + 1) * CAP], table[shift], _pick(chunks, (dom_index + shift) % dom_count)),
            "dom",
            pairs,
        )
        received.append(slab)
        maps.append(ids)
        parts.append(part)
    parts = jnp.stack(parts)
    own = _pick(parts, dom_index % dom_count)
    for source in range(1, dom_count):
        own = own + _pick(parts, (dom_index - source) % dom_count)
    gathered = [own]
    for shift in range(1, dom_count):
        pairs = [(i, (i + shift) % dom_count) for i in range(dom_count)]
        gathered.append(lax.ppermute(own, "dom", pairs))
    gathered = jnp.stack(gathered)
    weight_grad = jnp.concatenate(
        [_pick(gathered, (dom_index - k) % dom_count) for k in range(dom_count)], axis=0
    )
    node_grad = _combine(
        jnp.concatenate(maps), jnp.concatenate(received, axis=0), local_blocks
    ).reshape(node_rows, width)
    return (node_grad, weight_grad)


def solution(mesh):
    return jax.shard_map(
        shards,
        mesh=mesh,
        in_specs=(
            P(("dom", "loop"), None),
            P(("dom", "loop"), None),
            P(("dom", "loop"), None),
            P(),
            P(("dom", "loop"), None, None),
            P(("dom", "loop"), None),
            P(("dom", "loop"), None),
            P(("dom", "loop")),
        ),
        out_specs=(P(("dom", "loop"), None), P()),
        check_vma=False,
    )
```

```python
import math

import jax
import jax.numpy as jnp
from jax import lax
from jax.experimental import pallas as pl
from jax.experimental.pallas import tpu as pltpu
from jax.sharding import PartitionSpec as P

GROUP = 32
CAP = 4


def _spmm_kernel(rows_ref, slots_ref, cnt_ref, tv_ref, part_ref, extra_ref, out_ref):
    g = pl.program_id(0)
    count = cnt_ref[0]
    group, tile_size, _ = tv_ref.shape
    base = g * group
    body_rows = CAP * tile_size

    @pl.when(g == 0)
    def _():
        out_ref[:, :body_rows, :] = jnp.zeros(
            (out_ref.shape[0], body_rows, out_ref.shape[2]), out_ref.dtype
        )
        out_ref[:, body_rows:, :] = extra_ref[...]

    @pl.when(base < count)
    def _():
        for t in range(group):
            j = base + t
            r = rows_ref[j]
            c = slots_ref[j]
            term = lax.dot_general(
                tv_ref[t],
                part_ref[r],
                (((0,), (0,)), ((), ())),
                preferred_element_type=jnp.float32,
            )
            dest = c // CAP
            start = pl.multiple_of((c % CAP) * tile_size, tile_size)
            window = out_ref.at[dest, pl.ds(start, tile_size), :]
            window[...] += jnp.where(j < count, term, 0.0)


def _spmm(rows, slots, count, tile_values, partition, extra):
    tiles, tile_size, _ = tile_values.shape
    part_blocks, _, width = partition.shape
    dests, extra_rows, _ = extra.shape
    out_rows = CAP * tile_size + extra_rows
    group = math.gcd(tiles, GROUP)

    def tv_map(g, rows_ref, slots_ref, cnt_ref):
        last = jnp.maximum((cnt_ref[0] + group - 1) // group - 1, 0)
        return (jnp.minimum(g, last), 0, 0)

    def whole(g, rows_ref, slots_ref, cnt_ref):
        return (0, 0, 0)

    return pl.pallas_call(
        _spmm_kernel,
        out_shape=jax.ShapeDtypeStruct((dests, out_rows, width), jnp.float32),
        grid_spec=pltpu.PrefetchScalarGridSpec(
            num_scalar_prefetch=3,
            grid=(tiles // group,),
            in_specs=[
                pl.BlockSpec((group, tile_size, tile_size), tv_map),
                pl.BlockSpec((part_blocks, tile_size, width), whole),
                pl.BlockSpec((dests, extra_rows, width), whole),
            ],
            out_specs=pl.BlockSpec((dests, out_rows, width), whole),
        ),
        compiler_params=pltpu.CompilerParams(
            dimension_semantics=("arbitrary",),
            vmem_limit_bytes=50 * 1024 * 1024,
        ),
        cost_estimate=pl.CostEstimate(
            flops=2 * tiles * tile_size * tile_size * width,
            transcendentals=0,
            bytes_accessed=tiles * tile_size * tile_size * 2 + dests * out_rows * width * 4,
        ),
    )(rows, slots, count, tile_values, partition, extra)


def _combine_kernel(map_ref, recv_ref, out_ref):
    g = pl.program_id(0)
    tile_size = out_ref.shape[1]

    @pl.when(g == 0)
    def _():
        out_ref[...] = jnp.zeros(out_ref.shape, out_ref.dtype)

    for k in range(CAP):
        b = map_ref[g * CAP + k]
        out_ref[b] += recv_ref[0, k * tile_size:(k + 1) * tile_size, :]


def _combine(block_map, received, out_blocks, tile_size):
    total, _, width = received.shape

    def recv_map(g, map_ref):
        return (g, 0, 0)

    def whole(g, map_ref):
        return (0, 0, 0)

    return pl.pallas_call(
        _combine_kernel,
        out_shape=jax.ShapeDtypeStruct((out_blocks, tile_size, width), jnp.float32),
        grid_spec=pltpu.PrefetchScalarGridSpec(
            num_scalar_prefetch=1,
            grid=(total,),
            in_specs=[pl.BlockSpec((1, CAP * tile_size, width), recv_map)],
            out_specs=pl.BlockSpec((out_blocks, tile_size, width), whole),
        ),
        compiler_params=pltpu.CompilerParams(dimension_semantics=("arbitrary",)),
        cost_estimate=pl.CostEstimate(
            flops=total * CAP * tile_size * width,
            transcendentals=0,
            bytes_accessed=(total * CAP + out_blocks) * tile_size * width * 4,
        ),
    )(block_map, received)


def _pick(stacked, index):
    return lax.dynamic_index_in_dim(stacked, index, axis=0, keepdims=False)


def shards(cotangent, preact, aggregated, weight, tile_values, tile_rows, tile_cols, tile_counts):
    node_rows, width = cotangent.shape
    tile_size = tile_values.shape[1]
    dom_count = lax.axis_size("dom")
    loop_count = lax.axis_size("loop")
    dom_index = lax.axis_index("dom")
    loop_index = lax.axis_index("loop")
    total_nodes = node_rows * dom_count * loop_count
    local_blocks = node_rows // tile_size
    tile_total = tile_rows.shape[1]

    masked = jnp.where(preact > 0, cotangent, jnp.zeros_like(cotangent))
    weight_term = jnp.dot(aggregated.T, masked, preferred_element_type=jnp.float32) * (
        1.0 / math.sqrt(total_nodes)
    )
    projected = jnp.dot(masked, weight.T, preferred_element_type=jnp.float32).astype(jnp.bfloat16)

    pieces = [projected]
    terms = [weight_term]
    for shift in range(1, loop_count):
        pairs = [(i, (i + shift) % loop_count) for i in range(loop_count)]
        piece, term = lax.ppermute((projected, weight_term), "loop", pairs)
        pieces.append(piece)
        terms.append(term)
    partition = jnp.concatenate(pieces, axis=0).reshape(
        loop_count * local_blocks, tile_size, width
    )
    terms = jnp.stack(terms)
    loop_sum = _pick(terms, loop_index % loop_count)
    for source in range(1, loop_count):
        loop_sum = loop_sum + _pick(terms, (loop_index - source) % loop_count)

    rows = tile_rows[0]
    source_loop = rows // local_blocks
    rows = ((loop_index - source_loop) % loop_count) * local_blocks + rows % local_blocks

    cols = tile_cols[0]
    live = jnp.arange(tile_total, dtype=jnp.int32) < tile_counts[0]
    all_blocks = dom_count * local_blocks
    onehot = cols[:, None] == jnp.arange(all_blocks, dtype=jnp.int32)[None, :]
    present = jnp.any(onehot & live[:, None], axis=0).reshape(dom_count, local_blocks)
    present = present.astype(jnp.int32)
    rank = jnp.cumsum(present, axis=1) - 1
    tile_rank = jnp.sum(jnp.where(onehot, rank.reshape(1, -1), 0), axis=1)
    tile_rank = jnp.clip(tile_rank, 0, CAP - 1)
    block_ids = jnp.arange(local_blocks, dtype=jnp.int32)
    table = jnp.stack(
        [jnp.sum(jnp.where((rank == k) & (present > 0), block_ids[None, :], 0), axis=1) for k in range(CAP)],
        axis=1,
    )
    dom_ids = jnp.arange(dom_count, dtype=jnp.int32)
    rotate = ((dom_ids[:, None] + dom_index) % dom_count) == dom_ids[None, :]
    table = jnp.sum(jnp.where(rotate[:, :, None], table[None, :, :], 0), axis=1)
    dest_dom = cols // local_blocks
    slots = ((dest_dom - dom_index) % dom_count) * CAP + tile_rank

    chunk = width // dom_count
    chunks = loop_sum.reshape(dom_count, chunk, width)
    chunks = jnp.stack([_pick(chunks, (dom_index + shift) % dom_count) for shift in range(dom_count)])
    id_rows = jnp.zeros((dom_count, 8, width), jnp.float32)
    id_rows = id_rows.at[:, 0, :CAP].set(table.astype(jnp.float32))
    extra = jnp.concatenate([chunks, id_rows], axis=1)

    compact = _spmm(rows, slots, tile_counts, tile_values, partition, extra)

    received = [compact[0]]
    for shift in range(1, dom_count):
        pairs = [(i, (i + shift) % dom_count) for i in range(dom_count)]
        received.append(lax.ppermute(compact[shift], "dom", pairs))
    received = jnp.stack(received)
    body_rows = CAP * tile_size
    parts = received[:, body_rows:body_rows + chunk, :]
    block_map = received[:, body_rows + chunk, :CAP].astype(jnp.int32).reshape(-1)
    own = _pick(parts, dom_index % dom_count)
    for source in range(1, dom_count):
        own = own + _pick(parts, (dom_index - source) % dom_count)
    gathered = [own]
    for shift in range(1, dom_count):
        pairs = [(i, (i + shift) % dom_count) for i in range(dom_count)]
        gathered.append(lax.ppermute(own, "dom", pairs))
    gathered = jnp.stack(gathered)
    weight_grad = jnp.concatenate(
        [_pick(gathered, (dom_index - k) % dom_count) for k in range(dom_count)], axis=0
    )
    node_grad = _combine(block_map, received, local_blocks, tile_size).reshape(node_rows, width)
    return (node_grad, weight_grad)


def solution(mesh):
    return jax.shard_map(
        shards,
        mesh=mesh,
        in_specs=(
            P(("dom", "loop"), None),
            P(("dom", "loop"), None),
            P(("dom", "loop"), None),
            P(),
            P(("dom", "loop"), None, None),
            P(("dom", "loop"), None),
            P(("dom", "loop"), None),
            P(("dom", "loop")),
        ),
        out_specs=(P(("dom", "loop"), None), P()),
        check_vma=False,
    )
```

```python
import math

import jax
import jax.numpy as jnp
from jax import lax
from jax.experimental import pallas as pl
from jax.experimental.pallas import tpu as pltpu
from jax.sharding import PartitionSpec as P

GROUP = 32
CAP = 4


def _spmm_kernel(rows_ref, slots_ref, cnt_ref, tv_ref, part_ref, extra_ref, out_ref):
    g = pl.program_id(0)
    count = cnt_ref[0]
    group, tile_size, _ = tv_ref.shape
    base = g * group
    body_rows = CAP * tile_size

    @pl.when(g == 0)
    def _():
        out_ref[:, :body_rows, :] = jnp.zeros(
            (out_ref.shape[0], body_rows, out_ref.shape[2]), out_ref.dtype
        )
        out_ref[:, body_rows:, :] = extra_ref[...]

    @pl.when(base < count)
    def _():
        for t in range(group):
            j = base + t
            r = rows_ref[j]
            c = slots_ref[j]
            term = lax.dot_general(
                tv_ref[t],
                part_ref[r],
                (((0,), (0,)), ((), ())),
                preferred_element_type=jnp.float32,
            )
            dest = c // CAP
            start = pl.multiple_of((c % CAP) * tile_size, tile_size)
            window = out_ref.at[dest, pl.ds(start, tile_size), :]
            window[...] += jnp.where(j < count, term, 0.0)


def _spmm(rows, slots, count, tile_values, partition, extra):
    tiles, tile_size, _ = tile_values.shape
    part_blocks, _, width = partition.shape
    dests, extra_rows, _ = extra.shape
    out_rows = CAP * tile_size + extra_rows
    group = math.gcd(tiles, GROUP)

    def tv_map(g, rows_ref, slots_ref, cnt_ref):
        last = jnp.maximum((cnt_ref[0] + group - 1) // group - 1, 0)
        return (jnp.minimum(g, last), 0, 0)

    def whole(g, rows_ref, slots_ref, cnt_ref):
        return (0, 0, 0)

    return pl.pallas_call(
        _spmm_kernel,
        out_shape=jax.ShapeDtypeStruct((dests, out_rows, width), jnp.float32),
        grid_spec=pltpu.PrefetchScalarGridSpec(
            num_scalar_prefetch=3,
            grid=(tiles // group,),
            in_specs=[
                pl.BlockSpec((group, tile_size, tile_size), tv_map),
                pl.BlockSpec((part_blocks, tile_size, width), whole),
                pl.BlockSpec((dests, extra_rows, width), whole),
            ],
            out_specs=pl.BlockSpec((dests, out_rows, width), whole),
        ),
        compiler_params=pltpu.CompilerParams(
            dimension_semantics=("arbitrary",),
            vmem_limit_bytes=50 * 1024 * 1024,
        ),
        cost_estimate=pl.CostEstimate(
            flops=2 * tiles * tile_size * tile_size * width,
            transcendentals=0,
            bytes_accessed=tiles * tile_size * tile_size * 2 + dests * out_rows * width * 4,
        ),
    )(rows, slots, count, tile_values, partition, extra)


def _combine_kernel(map_ref, recv_ref, init_ref, out_ref):
    g = pl.program_id(0)
    tile_size = out_ref.shape[1]

    @pl.when(g == 0)
    def _():
        out_ref[...] = init_ref[...]

    for k in range(CAP):
        b = map_ref[g * CAP + k]
        out_ref[b] += recv_ref[0, k * tile_size:(k + 1) * tile_size, :]


def _combine(block_map, received, init):
    total, _, width = received.shape
    out_blocks, tile_size, _ = init.shape

    def recv_map(g, map_ref):
        return (g, 0, 0)

    def whole(g, map_ref):
        return (0, 0, 0)

    return pl.pallas_call(
        _combine_kernel,
        out_shape=jax.ShapeDtypeStruct((out_blocks, tile_size, width), jnp.float32),
        grid_spec=pltpu.PrefetchScalarGridSpec(
            num_scalar_prefetch=1,
            grid=(total,),
            in_specs=[
                pl.BlockSpec((1, CAP * tile_size, width), recv_map),
                pl.BlockSpec((out_blocks, tile_size, width), whole),
            ],
            out_specs=pl.BlockSpec((out_blocks, tile_size, width), whole),
        ),
        compiler_params=pltpu.CompilerParams(dimension_semantics=("arbitrary",)),
        cost_estimate=pl.CostEstimate(
            flops=total * CAP * tile_size * width,
            transcendentals=0,
            bytes_accessed=(total * CAP + 2 * out_blocks) * tile_size * width * 4,
        ),
    )(block_map, received, init)


def _pick(stacked, index):
    return lax.dynamic_index_in_dim(stacked, index, axis=0, keepdims=False)


def shards(cotangent, preact, aggregated, weight, tile_values, tile_rows, tile_cols, tile_counts):
    node_rows, width = cotangent.shape
    tile_size = tile_values.shape[1]
    dom_count = lax.axis_size("dom")
    loop_count = lax.axis_size("loop")
    dom_index = lax.axis_index("dom")
    loop_index = lax.axis_index("loop")
    total_nodes = node_rows * dom_count * loop_count
    local_blocks = node_rows // tile_size
    tile_total = tile_rows.shape[1]

    masked = jnp.where(preact > 0, cotangent, jnp.zeros_like(cotangent))
    weight_term = jnp.dot(aggregated.T, masked, preferred_element_type=jnp.float32) * (
        1.0 / math.sqrt(total_nodes)
    )
    projected = jnp.dot(masked, weight.T, preferred_element_type=jnp.float32).astype(jnp.bfloat16)

    pieces = [projected]
    terms = [weight_term]
    for shift in range(1, loop_count):
        pairs = [(i, (i + shift) % loop_count) for i in range(loop_count)]
        piece, term = lax.ppermute((projected, weight_term), "loop", pairs)
        pieces.append(piece)
        terms.append(term)
    partition = jnp.concatenate(pieces, axis=0).reshape(
        loop_count * local_blocks, tile_size, width
    )
    terms = jnp.stack(terms)
    loop_sum = _pick(terms, loop_index % loop_count)
    for source in range(1, loop_count):
        loop_sum = loop_sum + _pick(terms, (loop_index - source) % loop_count)

    rows = tile_rows[0]
    source_loop = rows // local_blocks
    rows = ((loop_index - source_loop) % loop_count) * local_blocks + rows % local_blocks

    cols = tile_cols[0]
    live = jnp.arange(tile_total, dtype=jnp.int32) < tile_counts[0]
    all_blocks = dom_count * local_blocks
    onehot = cols[:, None] == jnp.arange(all_blocks, dtype=jnp.int32)[None, :]
    present = jnp.any(onehot & live[:, None], axis=0).reshape(dom_count, local_blocks)
    present = present.astype(jnp.int32)
    rank = jnp.cumsum(present, axis=1) - 1
    tile_rank = jnp.sum(jnp.where(onehot, rank.reshape(1, -1), 0), axis=1)
    tile_rank = jnp.clip(tile_rank, 0, CAP - 1)
    block_ids = jnp.arange(local_blocks, dtype=jnp.int32)
    table = jnp.stack(
        [jnp.sum(jnp.where((rank == k) & (present > 0), block_ids[None, :], 0), axis=1) for k in range(CAP)],
        axis=1,
    )
    half = dom_count // 2
    side = dom_index // half
    pos = dom_index % half
    dest_dom = cols // local_blocks
    cross = (dest_dom // half != side).astype(jnp.int32)
    slots = (cross * half + (dest_dom % half - pos) % half) * CAP + tile_rank
    order = jnp.arange(dom_count, dtype=jnp.int32)
    order_side = jnp.where(order // half == 0, side, 1 - side)
    order = order_side * half + (pos + order % half) % half
    dom_ids = jnp.arange(dom_count, dtype=jnp.int32)
    rotate = order[:, None] == dom_ids[None, :]
    table = jnp.sum(jnp.where(rotate[:, :, None], table[None, :, :], 0), axis=1)

    chunk = width // dom_count
    chunks = loop_sum.reshape(dom_count, chunk, width)
    chunks = jnp.stack([_pick(chunks, order[i]) for i in range(dom_count)])
    id_rows = jnp.zeros((dom_count, 8, width), jnp.float32)
    id_rows = id_rows.at[:, 0, :CAP].set(table.astype(jnp.float32))
    extra = jnp.concatenate([chunks, id_rows], axis=1)

    compact = _spmm(rows, slots, tile_counts, tile_values, partition, extra)
    body_rows = CAP * tile_size

    def within(shift):
        return [(i, (i // half) * half + (i % half + shift) % half) for i in range(dom_count)]

    swap = [(i, (1 - i // half) * half + i % half) for i in range(dom_count)]

    def unpack(slabs):
        ids = slabs[:, body_rows + chunk, :CAP].astype(jnp.int32).reshape(-1)
        total = slabs[0, body_rows:body_rows + chunk, :]
        for k in range(1, slabs.shape[0]):
            total = total + slabs[k, body_rows:body_rows + chunk, :]
        return ids, total

    relay = [compact[half]]
    for shift in range(1, half):
        relay.append(lax.ppermute(compact[half + shift], "dom", within(shift)))
    relay = jnp.stack(relay)
    relay_ids, relay_chunk = unpack(relay)
    zeros = jnp.zeros((local_blocks, tile_size, width), jnp.float32)
    dense = _combine(relay_ids, relay, zeros)
    payload = jnp.concatenate([dense.reshape(node_rows, width), relay_chunk], axis=0)

    direct = [compact[shift] for shift in range(1, half)]
    direct, payload = lax.optimization_barrier((direct, payload))
    partner = lax.ppermute(payload, "dom", swap)
    received = [compact[0]]
    for shift in range(1, half):
        received.append(lax.ppermute(direct[shift - 1], "dom", within(shift)))
    received = jnp.stack(received)
    ids, own = unpack(received)
    own = own + partner[node_rows:]
    node_grad = _combine(ids, received, partner[:node_rows].reshape(local_blocks, tile_size, width))
    node_grad = node_grad.reshape(node_rows, width)

    gathered = [own]
    for shift in range(1, dom_count):
        pairs = [(i, (i + shift) % dom_count) for i in range(dom_count)]
        gathered.append(lax.ppermute(own, "dom", pairs))
    gathered = jnp.stack(gathered)
    weight_grad = jnp.concatenate(
        [_pick(gathered, (dom_index - k) % dom_count) for k in range(dom_count)], axis=0
    )
    return (node_grad, weight_grad)


def solution(mesh):
    return jax.shard_map(
        shards,
        mesh=mesh,
        in_specs=(
            P(("dom", "loop"), None),
            P(("dom", "loop"), None),
            P(("dom", "loop"), None),
            P(),
            P(("dom", "loop"), None, None),
            P(("dom", "loop"), None),
            P(("dom", "loop"), None),
            P(("dom", "loop")),
        ),
        out_specs=(P(("dom", "loop"), None), P()),
        check_vma=False,
    )
```

```python
import math

import jax
import jax.numpy as jnp
from jax import lax
from jax.experimental import pallas as pl
from jax.experimental.pallas import tpu as pltpu
from jax.sharding import PartitionSpec as P

GROUP = 32
CAP = 4


def _spmm_kernel(rows_ref, slots_ref, cnt_ref, tv_ref, part_ref, extra_ref, out_ref):
    g = pl.program_id(0)
    count = cnt_ref[0]
    group, tile_size, _ = tv_ref.shape
    base = g * group
    body_rows = CAP * tile_size

    @pl.when(g == 0)
    def _():
        out_ref[:, :body_rows, :] = jnp.zeros(
            (out_ref.shape[0], body_rows, out_ref.shape[2]), out_ref.dtype
        )
        out_ref[:, body_rows:, :] = extra_ref[...]

    @pl.when(base < count)
    def _():
        for t in range(group):
            j = base + t
            r = rows_ref[j]
            c = slots_ref[j]
            term = lax.dot_general(
                tv_ref[t],
                part_ref[r],
                (((0,), (0,)), ((), ())),
                preferred_element_type=jnp.float32,
            )
            dest = c // CAP
            start = pl.multiple_of((c % CAP) * tile_size, tile_size)
            window = out_ref.at[dest, pl.ds(start, tile_size), :]
            window[...] += jnp.where(j < count, term, 0.0)


def _spmm(rows, slots, count, tile_values, partition, extra):
    tiles, tile_size, _ = tile_values.shape
    part_blocks, _, width = partition.shape
    dests, extra_rows, _ = extra.shape
    out_rows = CAP * tile_size + extra_rows
    group = math.gcd(tiles, GROUP)

    def tv_map(g, rows_ref, slots_ref, cnt_ref):
        last = jnp.maximum((cnt_ref[0] + group - 1) // group - 1, 0)
        return (jnp.minimum(g, last), 0, 0)

    def whole(g, rows_ref, slots_ref, cnt_ref):
        return (0, 0, 0)

    return pl.pallas_call(
        _spmm_kernel,
        out_shape=jax.ShapeDtypeStruct((dests, out_rows, width), jnp.float32),
        grid_spec=pltpu.PrefetchScalarGridSpec(
            num_scalar_prefetch=3,
            grid=(tiles // group,),
            in_specs=[
                pl.BlockSpec((group, tile_size, tile_size), tv_map),
                pl.BlockSpec((part_blocks, tile_size, width), whole),
                pl.BlockSpec((dests, extra_rows, width), whole),
            ],
            out_specs=pl.BlockSpec((dests, out_rows, width), whole),
        ),
        compiler_params=pltpu.CompilerParams(
            dimension_semantics=("arbitrary",),
            vmem_limit_bytes=50 * 1024 * 1024,
        ),
        cost_estimate=pl.CostEstimate(
            flops=2 * tiles * tile_size * tile_size * width,
            transcendentals=0,
            bytes_accessed=tiles * tile_size * tile_size * 2 + dests * out_rows * width * 4,
        ),
    )(rows, slots, count, tile_values, partition, extra)


def _combine_kernel(map_ref, recv_ref, init_ref, out_ref):
    g = pl.program_id(0)
    tile_size = out_ref.shape[1]

    @pl.when(g == 0)
    def _():
        out_ref[...] = init_ref[...]

    for k in range(CAP):
        b = map_ref[g * CAP + k]
        out_ref[b] += recv_ref[0, k * tile_size:(k + 1) * tile_size, :]


def _combine(block_map, received, init):
    total, _, width = received.shape
    out_blocks, tile_size, _ = init.shape

    def recv_map(g, map_ref):
        return (g, 0, 0)

    def whole(g, map_ref):
        return (0, 0, 0)

    return pl.pallas_call(
        _combine_kernel,
        out_shape=jax.ShapeDtypeStruct((out_blocks, tile_size, width), jnp.float32),
        grid_spec=pltpu.PrefetchScalarGridSpec(
            num_scalar_prefetch=1,
            grid=(total,),
            in_specs=[
                pl.BlockSpec((1, CAP * tile_size, width), recv_map),
                pl.BlockSpec((out_blocks, tile_size, width), whole),
            ],
            out_specs=pl.BlockSpec((out_blocks, tile_size, width), whole),
        ),
        compiler_params=pltpu.CompilerParams(dimension_semantics=("arbitrary",)),
        cost_estimate=pl.CostEstimate(
            flops=total * CAP * tile_size * width,
            transcendentals=0,
            bytes_accessed=(total * CAP + 2 * out_blocks) * tile_size * width * 4,
        ),
    )(block_map, received, init)


def _pick(stacked, index):
    return lax.dynamic_index_in_dim(stacked, index, axis=0, keepdims=False)


def shards(cotangent, preact, aggregated, weight, tile_values, tile_rows, tile_cols, tile_counts):
    node_rows, width = cotangent.shape
    tile_size = tile_values.shape[1]
    dom_count = lax.axis_size("dom")
    loop_count = lax.axis_size("loop")
    dom_index = lax.axis_index("dom")
    loop_index = lax.axis_index("loop")
    total_nodes = node_rows * dom_count * loop_count
    local_blocks = node_rows // tile_size
    tile_total = tile_rows.shape[1]

    masked = jnp.where(preact > 0, cotangent, jnp.zeros_like(cotangent))
    weight_term = jnp.dot(aggregated.T, masked, preferred_element_type=jnp.float32) * (
        1.0 / math.sqrt(total_nodes)
    )
    projected = jnp.dot(masked, weight.T, preferred_element_type=jnp.float32).astype(jnp.bfloat16)

    pieces = [projected]
    for shift in range(1, loop_count):
        pairs = [(i, (i + shift) % loop_count) for i in range(loop_count)]
        pieces.append(lax.ppermute(projected, "loop", pairs))
    partition = jnp.concatenate(pieces, axis=0).reshape(
        loop_count * local_blocks, tile_size, width
    )
    partition, weight_term = lax.optimization_barrier((partition, weight_term))
    terms = [weight_term]
    for shift in range(1, loop_count):
        pairs = [(i, (i + shift) % loop_count) for i in range(loop_count)]
        terms.append(lax.ppermute(weight_term, "loop", pairs))
    terms = jnp.stack(terms)
    loop_sum = _pick(terms, loop_index % loop_count)
    for source in range(1, loop_count):
        loop_sum = loop_sum + _pick(terms, (loop_index - source) % loop_count)

    rows = tile_rows[0]
    source_loop = rows // local_blocks
    rows = ((loop_index - source_loop) % loop_count) * local_blocks + rows % local_blocks

    cols = tile_cols[0]
    live = jnp.arange(tile_total, dtype=jnp.int32) < tile_counts[0]
    all_blocks = dom_count * local_blocks
    onehot = cols[:, None] == jnp.arange(all_blocks, dtype=jnp.int32)[None, :]
    present = jnp.any(onehot & live[:, None], axis=0).reshape(dom_count, local_blocks)
    present = present.astype(jnp.int32)
    rank = jnp.cumsum(present, axis=1) - 1
    tile_rank = jnp.sum(jnp.where(onehot, rank.reshape(1, -1), 0), axis=1)
    tile_rank = jnp.clip(tile_rank, 0, CAP - 1)
    block_ids = jnp.arange(local_blocks, dtype=jnp.int32)
    table = jnp.stack(
        [jnp.sum(jnp.where((rank == k) & (present > 0), block_ids[None, :], 0), axis=1) for k in range(CAP)],
        axis=1,
    )
    half = dom_count // 2
    side = dom_index // half
    pos = dom_index % half
    dest_dom = cols // local_blocks
    cross = (dest_dom // half != side).astype(jnp.int32)
    slots = (cross * half + (dest_dom % half - pos) % half) * CAP + tile_rank
    order = jnp.arange(dom_count, dtype=jnp.int32)
    order_side = jnp.where(order // half == 0, side, 1 - side)
    order = order_side * half + (pos + order % half) % half
    dom_ids = jnp.arange(dom_count, dtype=jnp.int32)
    rotate = order[:, None] == dom_ids[None, :]
    table = jnp.sum(jnp.where(rotate[:, :, None], table[None, :, :], 0), axis=1)

    chunk = width // dom_count
    id_rows = jnp.zeros((dom_count, 8, width), jnp.float32)
    id_rows = id_rows.at[:, 0, :CAP].set(table.astype(jnp.float32))
    extra = jnp.concatenate([jnp.zeros((dom_count, 2 * chunk, width), jnp.float32), id_rows], axis=1)

    compact = _spmm(rows, slots, tile_counts, tile_values, partition, extra)
    body_rows = CAP * tile_size
    chunks = loop_sum.reshape(dom_count, chunk, width)
    first = jnp.stack([_pick(chunks, order[i]) for i in range(dom_count)])
    second = jnp.concatenate(
        [jnp.zeros((half, chunk, width), jnp.float32), first[:half]], axis=0
    )
    compact = lax.dynamic_update_slice(
        compact, jnp.concatenate([first, second], axis=1), (0, body_rows, 0)
    )

    def within(shift):
        return [(i, (i // half) * half + (i % half + shift) % half) for i in range(dom_count)]

    swap = [(i, (1 - i // half) * half + i % half) for i in range(dom_count)]

    def unpack(slabs):
        ids = slabs[:, body_rows + 2 * chunk, :CAP].astype(jnp.int32).reshape(-1)
        relayed = slabs[0, body_rows:body_rows + chunk, :]
        kept = slabs[0, body_rows + chunk:body_rows + 2 * chunk, :]
        for k in range(1, slabs.shape[0]):
            relayed = relayed + slabs[k, body_rows:body_rows + chunk, :]
            kept = kept + slabs[k, body_rows + chunk:body_rows + 2 * chunk, :]
        return ids, relayed, kept

    relay = [compact[half]]
    for shift in range(1, half):
        relay.append(lax.ppermute(compact[half + shift], "dom", within(shift)))
    relay = jnp.stack(relay)
    relay_ids, relay_chunk, own = unpack(relay)
    own = own + lax.ppermute(relay_chunk, "dom", swap)
    zeros = jnp.zeros((local_blocks, tile_size, width), jnp.float32)
    payload = _combine(relay_ids, relay, zeros)

    direct = [compact[shift] for shift in range(1, half)]
    direct, payload = lax.optimization_barrier((direct, payload))
    partner = lax.ppermute(payload, "dom", swap)
    received = [compact[0]]
    for shift in range(1, half):
        received.append(lax.ppermute(direct[shift - 1], "dom", within(shift)))
    received = jnp.stack(received)
    ids = received[:, body_rows + 2 * chunk, :CAP].astype(jnp.int32).reshape(-1)
    node_grad = _combine(ids, received, partner).reshape(node_rows, width)

    gathered = [own]
    for shift in range(1, dom_count):
        pairs = [(i, (i + shift) % dom_count) for i in range(dom_count)]
        gathered.append(lax.ppermute(own, "dom", pairs))
    gathered = jnp.stack(gathered)
    weight_grad = jnp.concatenate(
        [_pick(gathered, (dom_index - k) % dom_count) for k in range(dom_count)], axis=0
    )
    return (node_grad, weight_grad)


def solution(mesh):
    return jax.shard_map(
        shards,
        mesh=mesh,
        in_specs=(
            P(("dom", "loop"), None),
            P(("dom", "loop"), None),
            P(("dom", "loop"), None),
            P(),
            P(("dom", "loop"), None, None),
            P(("dom", "loop"), None),
            P(("dom", "loop"), None),
            P(("dom", "loop")),
        ),
        out_specs=(P(("dom", "loop"), None), P()),
        check_vma=False,
    )
```

```python
import math

import jax
import jax.numpy as jnp
from jax import lax
from jax.experimental import pallas as pl
from jax.experimental.pallas import tpu as pltpu
from jax.sharding import PartitionSpec as P

GROUP = 32
CAP = 4


def _spmm_kernel(rows_ref, slots_ref, cnt_ref, tv_ref, part_ref, extra_ref, out_ref):
    g = pl.program_id(0)
    count = cnt_ref[0]
    group, tile_size, _ = tv_ref.shape
    base = g * group
    body_rows = CAP * tile_size

    @pl.when(g == 0)
    def _():
        out_ref[:, :body_rows, :] = jnp.zeros(
            (out_ref.shape[0], body_rows, out_ref.shape[2]), out_ref.dtype
        )
        out_ref[:, body_rows:, :] = extra_ref[...]

    @pl.when(base < count)
    def _():
        for t in range(group):
            j = base + t
            r = rows_ref[j]
            c = slots_ref[j]
            term = lax.dot_general(
                tv_ref[t],
                part_ref[r],
                (((0,), (0,)), ((), ())),
                preferred_element_type=jnp.float32,
            )
            dest = c // CAP
            start = pl.multiple_of((c % CAP) * tile_size, tile_size)
            window = out_ref.at[dest, pl.ds(start, tile_size), :]
            window[...] += jnp.where(j < count, term, 0.0)


def _spmm(rows, slots, count, tile_values, partition, extra):
    tiles, tile_size, _ = tile_values.shape
    part_blocks, _, width = partition.shape
    dests, extra_rows, _ = extra.shape
    out_rows = CAP * tile_size + extra_rows
    group = math.gcd(tiles, GROUP)

    def tv_map(g, rows_ref, slots_ref, cnt_ref):
        last = jnp.maximum((cnt_ref[0] + group - 1) // group - 1, 0)
        return (jnp.minimum(g, last), 0, 0)

    def whole(g, rows_ref, slots_ref, cnt_ref):
        return (0, 0, 0)

    return pl.pallas_call(
        _spmm_kernel,
        out_shape=jax.ShapeDtypeStruct((dests, out_rows, width), jnp.float32),
        grid_spec=pltpu.PrefetchScalarGridSpec(
            num_scalar_prefetch=3,
            grid=(tiles // group,),
            in_specs=[
                pl.BlockSpec((group, tile_size, tile_size), tv_map),
                pl.BlockSpec((part_blocks, tile_size, width), whole),
                pl.BlockSpec((dests, extra_rows, width), whole),
            ],
            out_specs=pl.BlockSpec((dests, out_rows, width), whole),
        ),
        compiler_params=pltpu.CompilerParams(
            dimension_semantics=("arbitrary",),
            vmem_limit_bytes=50 * 1024 * 1024,
        ),
        cost_estimate=pl.CostEstimate(
            flops=2 * tiles * tile_size * tile_size * width,
            transcendentals=0,
            bytes_accessed=tiles * tile_size * tile_size * 2 + dests * out_rows * width * 4,
        ),
    )(rows, slots, count, tile_values, partition, extra)


def _combine_kernel(map_ref, recv_ref, init_ref, out_ref):
    g = pl.program_id(0)
    tile_size = out_ref.shape[1]

    @pl.when(g == 0)
    def _():
        out_ref[...] = init_ref[...]

    for k in range(CAP):
        b = map_ref[g * CAP + k]
        out_ref[b] += recv_ref[0, k * tile_size:(k + 1) * tile_size, :]


def _combine(block_map, received, init):
    total, _, width = received.shape
    out_blocks, tile_size, _ = init.shape

    def recv_map(g, map_ref):
        return (g, 0, 0)

    def whole(g, map_ref):
        return (0, 0, 0)

    return pl.pallas_call(
        _combine_kernel,
        out_shape=jax.ShapeDtypeStruct((out_blocks, tile_size, width), jnp.float32),
        grid_spec=pltpu.PrefetchScalarGridSpec(
            num_scalar_prefetch=1,
            grid=(total,),
            in_specs=[
                pl.BlockSpec((1, CAP * tile_size, width), recv_map),
                pl.BlockSpec((out_blocks, tile_size, width), whole),
            ],
            out_specs=pl.BlockSpec((out_blocks, tile_size, width), whole),
        ),
        compiler_params=pltpu.CompilerParams(dimension_semantics=("arbitrary",)),
        cost_estimate=pl.CostEstimate(
            flops=total * CAP * tile_size * width,
            transcendentals=0,
            bytes_accessed=(total * CAP + 2 * out_blocks) * tile_size * width * 4,
        ),
    )(block_map, received, init)


def _pick(stacked, index):
    return lax.dynamic_index_in_dim(stacked, index, axis=0, keepdims=False)


def shards(cotangent, preact, aggregated, weight, tile_values, tile_rows, tile_cols, tile_counts):
    node_rows, width = cotangent.shape
    tile_size = tile_values.shape[1]
    dom_count = lax.axis_size("dom")
    loop_count = lax.axis_size("loop")
    dom_index = lax.axis_index("dom")
    loop_index = lax.axis_index("loop")
    total_nodes = node_rows * dom_count * loop_count
    local_blocks = node_rows // tile_size
    tile_total = tile_rows.shape[1]

    masked = jnp.where(preact > 0, cotangent, jnp.zeros_like(cotangent))
    weight_term = jnp.dot(aggregated.T, masked, preferred_element_type=jnp.float32) * (
        1.0 / math.sqrt(total_nodes)
    )
    projected = jnp.dot(masked, weight.T, preferred_element_type=jnp.float32).astype(jnp.bfloat16)

    pieces = [projected]
    for shift in range(1, loop_count):
        pairs = [(i, (i + shift) % loop_count) for i in range(loop_count)]
        pieces.append(lax.ppermute(projected, "loop", pairs))
    partition = jnp.concatenate(pieces, axis=0).reshape(
        loop_count * local_blocks, tile_size, width
    )
    partition, weight_term = lax.optimization_barrier((partition, weight_term))
    terms = [weight_term]
    for shift in range(1, loop_count):
        pairs = [(i, (i + shift) % loop_count) for i in range(loop_count)]
        terms.append(lax.ppermute(weight_term, "loop", pairs))
    terms = jnp.stack(terms)
    loop_sum = _pick(terms, loop_index % loop_count)
    for source in range(1, loop_count):
        loop_sum = loop_sum + _pick(terms, (loop_index - source) % loop_count)

    rows = tile_rows[0]
    source_loop = rows // local_blocks
    rows = ((loop_index - source_loop) % loop_count) * local_blocks + rows % local_blocks

    cols = tile_cols[0]
    live = jnp.arange(tile_total, dtype=jnp.int32) < tile_counts[0]
    all_blocks = dom_count * local_blocks
    onehot = cols[:, None] == jnp.arange(all_blocks, dtype=jnp.int32)[None, :]
    present = jnp.any(onehot & live[:, None], axis=0).reshape(dom_count, local_blocks)
    present = present.astype(jnp.int32)
    rank = jnp.cumsum(present, axis=1) - 1
    tile_rank = jnp.sum(jnp.where(onehot, rank.reshape(1, -1), 0), axis=1)
    tile_rank = jnp.clip(tile_rank, 0, CAP - 1)
    block_ids = jnp.arange(local_blocks, dtype=jnp.int32)
    table = jnp.stack(
        [jnp.sum(jnp.where((rank == k) & (present > 0), block_ids[None, :], 0), axis=1) for k in range(CAP)],
        axis=1,
    )
    half = dom_count // 2
    side = dom_index // half
    pos = dom_index % half
    dest_dom = cols // local_blocks
    cross = (dest_dom // half != side).astype(jnp.int32)
    slots = (cross * half + (dest_dom % half - pos) % half) * CAP + tile_rank
    order = jnp.arange(dom_count, dtype=jnp.int32)
    order_side = jnp.where(order // half == 0, side, 1 - side)
    order = order_side * half + (pos + order % half) % half
    dom_ids = jnp.arange(dom_count, dtype=jnp.int32)
    rotate = order[:, None] == dom_ids[None, :]
    table = jnp.sum(jnp.where(rotate[:, :, None], table[None, :, :], 0), axis=1)

    chunk = width // dom_count
    id_rows = jnp.zeros((dom_count, 8, width), jnp.float32)
    id_rows = id_rows.at[:, 0, :CAP].set(table.astype(jnp.float32))
    extra = jnp.concatenate([jnp.zeros((dom_count, 2 * chunk, width), jnp.float32), id_rows], axis=1)

    compact = _spmm(rows, slots, tile_counts, tile_values, partition, extra)
    body_rows = CAP * tile_size
    chunks = loop_sum.reshape(dom_count, chunk, width)
    first = jnp.stack([_pick(chunks, order[i]) for i in range(dom_count)])
    second = jnp.concatenate(
        [jnp.zeros((half, chunk, width), jnp.float32), first[:half]], axis=0
    )
    compact = lax.dynamic_update_slice(
        compact, jnp.concatenate([first, second], axis=1), (0, body_rows, 0)
    )

    def within(shift):
        return [(i, (i // half) * half + (i % half + shift) % half) for i in range(dom_count)]

    swap = [(i, (1 - i // half) * half + i % half) for i in range(dom_count)]

    def unpack(slabs):
        ids = slabs[:, body_rows + 2 * chunk, :CAP].astype(jnp.int32).reshape(-1)
        relayed = slabs[0, body_rows:body_rows + chunk, :]
        kept = slabs[0, body_rows + chunk:body_rows + 2 * chunk, :]
        for k in range(1, slabs.shape[0]):
            relayed = relayed + slabs[k, body_rows:body_rows + chunk, :]
            kept = kept + slabs[k, body_rows + chunk:body_rows + 2 * chunk, :]
        return ids, relayed, kept

    relay = [compact[half]]
    for shift in range(1, half):
        relay.append(lax.ppermute(compact[half + shift], "dom", within(shift)))
    relay = jnp.stack(relay)
    relay_ids, relay_chunk, own = unpack(relay)
    own = own + lax.ppermute(relay_chunk, "dom", swap)
    zeros = jnp.zeros((local_blocks, tile_size, width), jnp.float32)
    payload = _combine(relay_ids, relay, zeros)

    held = [own]
    for shift in range(1, half):
        held.append(lax.ppermute(own, "dom", within(shift)))
    held = jnp.stack(held)
    half_chunks = jnp.concatenate(
        [_pick(held, (pos - q) % half) for q in range(half)], axis=0
    )
    payload = jnp.concatenate([payload.reshape(node_rows, width), half_chunks], axis=0)

    direct = [compact[shift] for shift in range(1, half)]
    direct, payload = lax.optimization_barrier((direct, payload))
    partner = lax.ppermute(payload, "dom", swap)
    received = [compact[0]]
    for shift in range(1, half):
        received.append(lax.ppermute(direct[shift - 1], "dom", within(shift)))
    received = jnp.stack(received)
    ids = received[:, body_rows + 2 * chunk, :CAP].astype(jnp.int32).reshape(-1)
    dense = partner[:node_rows].reshape(local_blocks, tile_size, width)
    node_grad = _combine(ids, received, dense).reshape(node_rows, width)
    other_chunks = partner[node_rows:]
    weight_grad = jnp.where(
        side == 0,
        jnp.concatenate([half_chunks, other_chunks], axis=0),
        jnp.concatenate([other_chunks, half_chunks], axis=0),
    )
    return (node_grad, weight_grad)


def solution(mesh):
    return jax.shard_map(
        shards,
        mesh=mesh,
        in_specs=(
            P(("dom", "loop"), None),
            P(("dom", "loop"), None),
            P(("dom", "loop"), None),
            P(),
            P(("dom", "loop"), None, None),
            P(("dom", "loop"), None),
            P(("dom", "loop"), None),
            P(("dom", "loop")),
        ),
        out_specs=(P(("dom", "loop"), None), P()),
        check_vma=False,
    )
```

```python
import math

import jax
import jax.numpy as jnp
from jax import lax
from jax.experimental import pallas as pl
from jax.experimental.pallas import tpu as pltpu
from jax.sharding import PartitionSpec as P

GROUP = 32
CAP = 4


def _spmm_kernel(rows_ref, slots_ref, cnt_ref, tv_ref, part_ref, extra_ref, out_ref):
    g = pl.program_id(0)
    count = cnt_ref[0]
    group, tile_size, _ = tv_ref.shape
    base = g * group
    body_rows = CAP * tile_size

    @pl.when(g == 0)
    def _():
        out_ref[:, :body_rows, :] = jnp.zeros(
            (out_ref.shape[0], body_rows, out_ref.shape[2]), out_ref.dtype
        )
        out_ref[:, body_rows:, :] = extra_ref[...]

    @pl.when(base < count)
    def _():
        for t in range(group):
            j = base + t
            r = rows_ref[j]
            c = slots_ref[j]
            term = lax.dot_general(
                tv_ref[t],
                part_ref[r],
                (((0,), (0,)), ((), ())),
                preferred_element_type=jnp.float32,
            )
            dest = c // CAP
            start = pl.multiple_of((c % CAP) * tile_size, tile_size)
            window = out_ref.at[dest, pl.ds(start, tile_size), :]
            window[...] += jnp.where(j < count, term, 0.0)


def _spmm(rows, slots, count, tile_values, partition, extra):
    tiles, tile_size, _ = tile_values.shape
    part_blocks, _, width = partition.shape
    dests, extra_rows, _ = extra.shape
    out_rows = CAP * tile_size + extra_rows
    group = math.gcd(tiles, GROUP)

    def tv_map(g, rows_ref, slots_ref, cnt_ref):
        last = jnp.maximum((cnt_ref[0] + group - 1) // group - 1, 0)
        return (jnp.minimum(g, last), 0, 0)

    def whole(g, rows_ref, slots_ref, cnt_ref):
        return (0, 0, 0)

    return pl.pallas_call(
        _spmm_kernel,
        out_shape=jax.ShapeDtypeStruct((dests, out_rows, width), jnp.float32),
        grid_spec=pltpu.PrefetchScalarGridSpec(
            num_scalar_prefetch=3,
            grid=(tiles // group,),
            in_specs=[
                pl.BlockSpec((group, tile_size, tile_size), tv_map),
                pl.BlockSpec((part_blocks, tile_size, width), whole),
                pl.BlockSpec((dests, extra_rows, width), whole),
            ],
            out_specs=pl.BlockSpec((dests, out_rows, width), whole),
        ),
        compiler_params=pltpu.CompilerParams(
            dimension_semantics=("arbitrary",),
            vmem_limit_bytes=50 * 1024 * 1024,
        ),
        cost_estimate=pl.CostEstimate(
            flops=2 * tiles * tile_size * tile_size * width,
            transcendentals=0,
            bytes_accessed=tiles * tile_size * tile_size * 2 + dests * out_rows * width * 4,
        ),
    )(rows, slots, count, tile_values, partition, extra)


def _combine_kernel(map_ref, *refs):
    slab_refs = refs[:-2]
    init_ref, out_ref = refs[-2:]
    out_blocks, tile_size, width = out_ref.shape
    out_ref[...] = init_ref[...].reshape(out_blocks, tile_size, width)
    for n, slab_ref in enumerate(slab_refs):
        for k in range(CAP):
            b = map_ref[n * CAP + k]
            out_ref[b] += slab_ref[k * tile_size:(k + 1) * tile_size, :]


def _combine(block_map, slabs, init, out_blocks, tile_size):
    rows, width = slabs[0].shape

    def whole(g, map_ref):
        return (0, 0)

    def out_map(g, map_ref):
        return (0, 0, 0)

    return pl.pallas_call(
        _combine_kernel,
        out_shape=jax.ShapeDtypeStruct((out_blocks, tile_size, width), jnp.float32),
        grid_spec=pltpu.PrefetchScalarGridSpec(
            num_scalar_prefetch=1,
            grid=(1,),
            in_specs=[pl.BlockSpec((rows, width), whole) for _ in slabs]
            + [pl.BlockSpec((out_blocks * tile_size, width), whole)],
            out_specs=pl.BlockSpec((out_blocks, tile_size, width), out_map),
        ),
        compiler_params=pltpu.CompilerParams(dimension_semantics=("arbitrary",)),
        cost_estimate=pl.CostEstimate(
            flops=len(slabs) * CAP * tile_size * width,
            transcendentals=0,
            bytes_accessed=(len(slabs) * CAP + 2 * out_blocks) * tile_size * width * 4,
        ),
    )(block_map, *slabs, init)


def _pick(stacked, index):
    return lax.dynamic_index_in_dim(stacked, index, axis=0, keepdims=False)


def shards(cotangent, preact, aggregated, weight, tile_values, tile_rows, tile_cols, tile_counts):
    node_rows, width = cotangent.shape
    tile_size = tile_values.shape[1]
    dom_count = lax.axis_size("dom")
    loop_count = lax.axis_size("loop")
    dom_index = lax.axis_index("dom")
    loop_index = lax.axis_index("loop")
    total_nodes = node_rows * dom_count * loop_count
    local_blocks = node_rows // tile_size
    tile_total = tile_rows.shape[1]

    masked = jnp.where(preact > 0, cotangent, jnp.zeros_like(cotangent))
    weight_term = jnp.dot(aggregated.T, masked, preferred_element_type=jnp.float32) * (
        1.0 / math.sqrt(total_nodes)
    )
    projected = jnp.dot(masked, weight.T, preferred_element_type=jnp.float32).astype(jnp.bfloat16)

    pieces = [projected]
    for shift in range(1, loop_count):
        pairs = [(i, (i + shift) % loop_count) for i in range(loop_count)]
        pieces.append(lax.ppermute(projected, "loop", pairs))
    partition = jnp.concatenate(pieces, axis=0).reshape(
        loop_count * local_blocks, tile_size, width
    )
    partition, weight_term = lax.optimization_barrier((partition, weight_term))
    terms = [weight_term]
    for shift in range(1, loop_count):
        pairs = [(i, (i + shift) % loop_count) for i in range(loop_count)]
        terms.append(lax.ppermute(weight_term, "loop", pairs))
    terms = jnp.stack(terms)
    loop_sum = _pick(terms, loop_index % loop_count)
    for source in range(1, loop_count):
        loop_sum = loop_sum + _pick(terms, (loop_index - source) % loop_count)

    rows = tile_rows[0]
    source_loop = rows // local_blocks
    rows = ((loop_index - source_loop) % loop_count) * local_blocks + rows % local_blocks

    cols = tile_cols[0]
    live = jnp.arange(tile_total, dtype=jnp.int32) < tile_counts[0]
    all_blocks = dom_count * local_blocks
    onehot = cols[:, None] == jnp.arange(all_blocks, dtype=jnp.int32)[None, :]
    present = jnp.any(onehot & live[:, None], axis=0).reshape(dom_count, local_blocks)
    present = present.astype(jnp.int32)
    rank = jnp.cumsum(present, axis=1) - 1
    tile_rank = jnp.sum(jnp.where(onehot, rank.reshape(1, -1), 0), axis=1)
    tile_rank = jnp.clip(tile_rank, 0, CAP - 1)
    block_ids = jnp.arange(local_blocks, dtype=jnp.int32)
    table = jnp.stack(
        [jnp.sum(jnp.where((rank == k) & (present > 0), block_ids[None, :], 0), axis=1) for k in range(CAP)],
        axis=1,
    )
    half = dom_count // 2
    side = dom_index // half
    pos = dom_index % half
    dest_dom = cols // local_blocks
    cross = (dest_dom // half != side).astype(jnp.int32)
    slots = (cross * half + (dest_dom % half - pos) % half) * CAP + tile_rank
    order = jnp.arange(dom_count, dtype=jnp.int32)
    order_side = jnp.where(order // half == 0, side, 1 - side)
    order = order_side * half + (pos + order % half) % half
    dom_ids = jnp.arange(dom_count, dtype=jnp.int32)
    rotate = order[:, None] == dom_ids[None, :]
    table = jnp.sum(jnp.where(rotate[:, :, None], table[None, :, :], 0), axis=1)

    id_rows = jnp.zeros((dom_count, 8, width), jnp.float32)
    extra = id_rows.at[:, 0, :CAP].set(table.astype(jnp.float32))

    compact = _spmm(rows, slots, tile_counts, tile_values, partition, extra)
    body_rows = CAP * tile_size
    chunk = width // dom_count
    chunks = loop_sum.reshape(dom_count, chunk, width)
    first = [_pick(chunks, order[half + i]) for i in range(half)]
    second = [_pick(chunks, order[i]) for i in range(half)]

    def within(shift):
        return [(i, (i // half) * half + (i % half + shift) % half) for i in range(dom_count)]

    swap = [(i, (1 - i // half) * half + i % half) for i in range(dom_count)]

    def ids_of(slabs):
        return jnp.concatenate([slab[body_rows, :CAP] for slab in slabs]).astype(jnp.int32)

    relay = [compact[half]]
    relay_chunk = first[0]
    own = second[0]
    for shift in range(1, half):
        slab, pair = lax.ppermute(
            (compact[half + shift], jnp.stack([first[shift], second[shift]])), "dom", within(shift)
        )
        relay.append(slab)
        relay_chunk = relay_chunk + pair[0]
        own = own + pair[1]
    own = own + lax.ppermute(relay_chunk, "dom", swap)
    zeros = jnp.zeros((local_blocks * tile_size, width), jnp.float32)
    payload = _combine(ids_of(relay), relay, zeros, local_blocks, tile_size)

    held = [own]
    for shift in range(1, half):
        held.append(lax.ppermute(own, "dom", within(shift)))
    held = jnp.stack(held)
    half_chunks = jnp.concatenate(
        [_pick(held, (pos - q) % half) for q in range(half)], axis=0
    )
    payload = jnp.concatenate([payload.reshape(node_rows, width), half_chunks], axis=0)

    direct = [compact[shift] for shift in range(1, half)]
    direct, payload = lax.optimization_barrier((direct, payload))
    partner = lax.ppermute(payload, "dom", swap)
    received = [compact[0]]
    for shift in range(1, half):
        received.append(lax.ppermute(direct[shift - 1], "dom", within(shift)))
    node_grad = _combine(ids_of(received), received, partner, local_blocks, tile_size)
    node_grad = node_grad.reshape(node_rows, width)
    other_chunks = partner[node_rows:]
    weight_grad = jnp.where(
        side == 0,
        jnp.concatenate([half_chunks, other_chunks], axis=0),
        jnp.concatenate([other_chunks, half_chunks], axis=0),
    )
    return (node_grad, weight_grad)


def solution(mesh):
    return jax.shard_map(
        shards,
        mesh=mesh,
        in_specs=(
            P(("dom", "loop"), None),
            P(("dom", "loop"), None),
            P(("dom", "loop"), None),
            P(),
            P(("dom", "loop"), None, None),
            P(("dom", "loop"), None),
            P(("dom", "loop"), None),
            P(("dom", "loop")),
        ),
        out_specs=(P(("dom", "loop"), None), P()),
        check_vma=False,
    )
```

```python
import math

import jax
import jax.numpy as jnp
from jax import lax
from jax.experimental import pallas as pl
from jax.experimental.pallas import tpu as pltpu
from jax.sharding import PartitionSpec as P

GROUP = 32
CAP = 4


def _spmm_kernel(rows_ref, slots_ref, cnt_ref, tv_ref, part_ref, extra_ref, out_ref):
    g = pl.program_id(0)
    count = cnt_ref[0]
    group, tile_size, _ = tv_ref.shape
    base = g * group
    body_rows = CAP * tile_size

    @pl.when(g == 0)
    def _():
        out_ref[:, :body_rows, :] = jnp.zeros(
            (out_ref.shape[0], body_rows, out_ref.shape[2]), out_ref.dtype
        )
        out_ref[:, body_rows:, :] = extra_ref[...]

    @pl.when(base < count)
    def _():
        for t in range(group):
            j = base + t
            r = rows_ref[j]
            c = slots_ref[j]
            term = lax.dot_general(
                tv_ref[t],
                part_ref[r],
                (((0,), (0,)), ((), ())),
                preferred_element_type=jnp.float32,
            )
            dest = c // CAP
            start = pl.multiple_of((c % CAP) * tile_size, tile_size)
            window = out_ref.at[dest, pl.ds(start, tile_size), :]
            window[...] += jnp.where(j < count, term, 0.0)


def _spmm(rows, slots, count, tile_values, partition, extra):
    tiles, tile_size, _ = tile_values.shape
    part_blocks, _, width = partition.shape
    dests, extra_rows, _ = extra.shape
    out_rows = CAP * tile_size + extra_rows
    group = math.gcd(tiles, GROUP)

    def tv_map(g, rows_ref, slots_ref, cnt_ref):
        last = jnp.maximum((cnt_ref[0] + group - 1) // group - 1, 0)
        return (jnp.minimum(g, last), 0, 0)

    def whole(g, rows_ref, slots_ref, cnt_ref):
        return (0, 0, 0)

    return pl.pallas_call(
        _spmm_kernel,
        out_shape=jax.ShapeDtypeStruct((dests, out_rows, width), jnp.float32),
        grid_spec=pltpu.PrefetchScalarGridSpec(
            num_scalar_prefetch=3,
            grid=(tiles // group,),
            in_specs=[
                pl.BlockSpec((group, tile_size, tile_size), tv_map),
                pl.BlockSpec((part_blocks, tile_size, width), whole),
                pl.BlockSpec((dests, extra_rows, width), whole),
            ],
            out_specs=pl.BlockSpec((dests, out_rows, width), whole),
        ),
        compiler_params=pltpu.CompilerParams(
            dimension_semantics=("arbitrary",),
            vmem_limit_bytes=50 * 1024 * 1024,
        ),
        cost_estimate=pl.CostEstimate(
            flops=2 * tiles * tile_size * tile_size * width,
            transcendentals=0,
            bytes_accessed=tiles * tile_size * tile_size * 2 + dests * out_rows * width * 4,
        ),
    )(rows, slots, count, tile_values, partition, extra)


def _combine_kernel(map_ref, *refs):
    slab_refs = refs[:-2]
    init_ref, out_ref = refs[-2:]
    out_blocks, tile_size, width = out_ref.shape
    out_ref[...] = init_ref[...].reshape(out_blocks, tile_size, width)
    for n, slab_ref in enumerate(slab_refs):
        for k in range(CAP):
            b = map_ref[n * CAP + k]
            out_ref[b] += slab_ref[k * tile_size:(k + 1) * tile_size, :]


def _combine(block_map, slabs, init, out_blocks, tile_size):
    rows, width = slabs[0].shape

    def whole(g, map_ref):
        return (0, 0)

    def out_map(g, map_ref):
        return (0, 0, 0)

    return pl.pallas_call(
        _combine_kernel,
        out_shape=jax.ShapeDtypeStruct((out_blocks, tile_size, width), jnp.float32),
        grid_spec=pltpu.PrefetchScalarGridSpec(
            num_scalar_prefetch=1,
            grid=(1,),
            in_specs=[pl.BlockSpec((rows, width), whole) for _ in slabs]
            + [pl.BlockSpec((out_blocks * tile_size, width), whole)],
            out_specs=pl.BlockSpec((out_blocks, tile_size, width), out_map),
        ),
        compiler_params=pltpu.CompilerParams(dimension_semantics=("arbitrary",)),
        cost_estimate=pl.CostEstimate(
            flops=len(slabs) * CAP * tile_size * width,
            transcendentals=0,
            bytes_accessed=(len(slabs) * CAP + 2 * out_blocks) * tile_size * width * 4,
        ),
    )(block_map, *slabs, init)


def _pick(stacked, index):
    return lax.dynamic_index_in_dim(stacked, index, axis=0, keepdims=False)


def shards(cotangent, preact, aggregated, weight, tile_values, tile_rows, tile_cols, tile_counts):
    node_rows, width = cotangent.shape
    tile_size = tile_values.shape[1]
    dom_count = lax.axis_size("dom")
    loop_count = lax.axis_size("loop")
    dom_index = lax.axis_index("dom")
    loop_index = lax.axis_index("loop")
    total_nodes = node_rows * dom_count * loop_count
    local_blocks = node_rows // tile_size
    tile_total = tile_rows.shape[1]

    masked = jnp.where(preact > 0, cotangent, jnp.zeros_like(cotangent))
    weight_term = jnp.dot(aggregated.T, masked, preferred_element_type=jnp.float32) * (
        1.0 / math.sqrt(total_nodes)
    )
    projected = jnp.dot(masked, weight.T, preferred_element_type=jnp.float32).astype(jnp.bfloat16)

    pieces = [projected]
    for shift in range(1, loop_count):
        pairs = [(i, (i + shift) % loop_count) for i in range(loop_count)]
        pieces.append(lax.ppermute(projected, "loop", pairs))
    partition = jnp.concatenate(pieces, axis=0).reshape(
        loop_count * local_blocks, tile_size, width
    )
    partition, weight_term = lax.optimization_barrier((partition, weight_term))
    terms = [weight_term]
    for shift in range(1, loop_count):
        pairs = [(i, (i + shift) % loop_count) for i in range(loop_count)]
        terms.append(lax.ppermute(weight_term, "loop", pairs))
    terms = jnp.stack(terms)
    loop_sum = _pick(terms, loop_index % loop_count)
    for source in range(1, loop_count):
        loop_sum = loop_sum + _pick(terms, (loop_index - source) % loop_count)

    rows = tile_rows[0]
    source_loop = rows // local_blocks
    rows = ((loop_index - source_loop) % loop_count) * local_blocks + rows % local_blocks

    cols = tile_cols[0]
    live = jnp.arange(tile_total, dtype=jnp.int32) < tile_counts[0]
    all_blocks = dom_count * local_blocks
    onehot = cols[:, None] == jnp.arange(all_blocks, dtype=jnp.int32)[None, :]
    present = jnp.any(onehot & live[:, None], axis=0).reshape(dom_count, local_blocks)
    present = present.astype(jnp.int32)
    rank = jnp.cumsum(present, axis=1) - 1
    tile_rank = jnp.sum(jnp.where(onehot, rank.reshape(1, -1), 0), axis=1)
    tile_rank = jnp.clip(tile_rank, 0, CAP - 1)
    block_ids = jnp.arange(local_blocks, dtype=jnp.int32)
    table = jnp.stack(
        [jnp.sum(jnp.where((rank == k) & (present > 0), block_ids[None, :], 0), axis=1) for k in range(CAP)],
        axis=1,
    )
    half = dom_count // 2
    side = dom_index // half
    pos = dom_index % half
    dest_dom = cols // local_blocks
    cross = (dest_dom // half != side).astype(jnp.int32)
    slots = (cross * half + (dest_dom % half - pos) % half) * CAP + tile_rank
    order = jnp.arange(dom_count, dtype=jnp.int32)
    order_side = jnp.where(order // half == 0, side, 1 - side)
    order = order_side * half + (pos + order % half) % half
    dom_ids = jnp.arange(dom_count, dtype=jnp.int32)
    rotate = order[:, None] == dom_ids[None, :]
    table = jnp.sum(jnp.where(rotate[:, :, None], table[None, :, :], 0), axis=1)

    chunk = width // dom_count
    id_rows = jnp.zeros((dom_count, 8, width), jnp.float32)
    id_rows = id_rows.at[:, 0, :CAP].set(table.astype(jnp.float32))
    extra = jnp.concatenate([jnp.zeros((dom_count, 2 * chunk, width), jnp.float32), id_rows], axis=1)

    compact = _spmm(rows, slots, tile_counts, tile_values, partition, extra)
    body_rows = CAP * tile_size
    chunks = loop_sum.reshape(dom_count, chunk, width)
    first = jnp.stack([_pick(chunks, order[i]) for i in range(dom_count)])
    second = jnp.concatenate(
        [jnp.zeros((half, chunk, width), jnp.float32), first[:half]], axis=0
    )
    compact = lax.dynamic_update_slice(
        compact, jnp.concatenate([first, second], axis=1), (0, body_rows, 0)
    )

    def within(shift):
        return [(i, (i // half) * half + (i % half + shift) % half) for i in range(dom_count)]

    swap = [(i, (1 - i // half) * half + i % half) for i in range(dom_count)]

    def ids_of(slabs):
        return jnp.concatenate([slab[body_rows + 2 * chunk, :CAP] for slab in slabs]).astype(jnp.int32)

    relay = [compact[half]]
    for shift in range(1, half):
        relay.append(lax.ppermute(compact[half + shift], "dom", within(shift)))
    relay_chunk = relay[0][body_rows:body_rows + chunk]
    own = relay[0][body_rows + chunk:body_rows + 2 * chunk]
    for slab in relay[1:]:
        relay_chunk = relay_chunk + slab[body_rows:body_rows + chunk]
        own = own + slab[body_rows + chunk:body_rows + 2 * chunk]
    own = own + lax.ppermute(relay_chunk, "dom", swap)
    zeros = jnp.zeros((local_blocks * tile_size, width), jnp.float32)
    payload = _combine(ids_of(relay), relay, zeros, local_blocks, tile_size)

    held = [own]
    for shift in range(1, half):
        held.append(lax.ppermute(own, "dom", within(shift)))
    held = jnp.stack(held)
    half_chunks = jnp.concatenate(
        [_pick(held, (pos - q) % half) for q in range(half)], axis=0
    )
    payload = jnp.concatenate([payload.reshape(node_rows, width), half_chunks], axis=0)

    direct = [compact[shift] for shift in range(1, half)]
    direct, payload = lax.optimization_barrier((direct, payload))
    partner = lax.ppermute(payload, "dom", swap)
    received = [compact[0]]
    for shift in range(1, half):
        received.append(lax.ppermute(direct[shift - 1], "dom", within(shift)))
    node_grad = _combine(ids_of(received), received, partner, local_blocks, tile_size)
    node_grad = node_grad.reshape(node_rows, width)
    other_chunks = partner[node_rows:]
    weight_grad = jnp.where(
        side == 0,
        jnp.concatenate([half_chunks, other_chunks], axis=0),
        jnp.concatenate([other_chunks, half_chunks], axis=0),
    )
    return (node_grad, weight_grad)


def solution(mesh):
    return jax.shard_map(
        shards,
        mesh=mesh,
        in_specs=(
            P(("dom", "loop"), None),
            P(("dom", "loop"), None),
            P(("dom", "loop"), None),
            P(),
            P(("dom", "loop"), None, None),
            P(("dom", "loop"), None),
            P(("dom", "loop"), None),
            P(("dom", "loop")),
        ),
        out_specs=(P(("dom", "loop"), None), P()),
        check_vma=False,
    )
```

```python
import math

import jax
import jax.numpy as jnp
from jax import lax
from jax.experimental import pallas as pl
from jax.experimental.pallas import tpu as pltpu
from jax.sharding import PartitionSpec as P

GROUP = 32
CAP = 4


def _spmm_kernel(rows_ref, slots_ref, cnt_ref, tv_ref, part_ref, extra_ref, out_ref):
    g = pl.program_id(0)
    count = cnt_ref[0]
    group, tile_size, _ = tv_ref.shape
    base = g * group
    body_rows = CAP * tile_size

    @pl.when(g == 0)
    def _():
        out_ref[:, :body_rows, :] = jnp.zeros(
            (out_ref.shape[0], body_rows, out_ref.shape[2]), out_ref.dtype
        )
        out_ref[:, body_rows:, :] = extra_ref[...]

    @pl.when(base < count)
    def _():
        for t in range(group):
            j = base + t
            r = rows_ref[j]
            c = slots_ref[j]
            term = lax.dot_general(
                tv_ref[t],
                part_ref[r],
                (((0,), (0,)), ((), ())),
                preferred_element_type=jnp.float32,
            )
            dest = c // CAP
            start = pl.multiple_of((c % CAP) * tile_size, tile_size)
            window = out_ref.at[dest, pl.ds(start, tile_size), :]
            window[...] += jnp.where(j < count, term, 0.0)


def _spmm(rows, slots, count, tile_values, partition, extra):
    tiles, tile_size, _ = tile_values.shape
    part_blocks, _, width = partition.shape
    dests, extra_rows, _ = extra.shape
    out_rows = CAP * tile_size + extra_rows
    group = math.gcd(tiles, GROUP)

    def tv_map(g, rows_ref, slots_ref, cnt_ref):
        last = jnp.maximum((cnt_ref[0] + group - 1) // group - 1, 0)
        return (jnp.minimum(g, last), 0, 0)

    def whole(g, rows_ref, slots_ref, cnt_ref):
        return (0, 0, 0)

    return pl.pallas_call(
        _spmm_kernel,
        out_shape=jax.ShapeDtypeStruct((dests, out_rows, width), jnp.float32),
        grid_spec=pltpu.PrefetchScalarGridSpec(
            num_scalar_prefetch=3,
            grid=(tiles // group,),
            in_specs=[
                pl.BlockSpec((group, tile_size, tile_size), tv_map),
                pl.BlockSpec((part_blocks, tile_size, width), whole),
                pl.BlockSpec((dests, extra_rows, width), whole),
            ],
            out_specs=pl.BlockSpec((dests, out_rows, width), whole),
        ),
        compiler_params=pltpu.CompilerParams(
            dimension_semantics=("arbitrary",),
            vmem_limit_bytes=50 * 1024 * 1024,
        ),
        cost_estimate=pl.CostEstimate(
            flops=2 * tiles * tile_size * tile_size * width,
            transcendentals=0,
            bytes_accessed=tiles * tile_size * tile_size * 2 + dests * out_rows * width * 4,
        ),
    )(rows, slots, count, tile_values, partition, extra)


def _combine_kernel(map_ref, *refs):
    slab_refs = refs[:-2]
    init_ref, out_ref = refs[-2:]
    out_blocks, tile_size, width = out_ref.shape
    out_ref[...] = init_ref[...].reshape(out_blocks, tile_size, width)
    for n, slab_ref in enumerate(slab_refs):
        for k in range(CAP):
            b = map_ref[n * CAP + k]
            out_ref[b] += slab_ref[k * tile_size:(k + 1) * tile_size, :]


def _combine(block_map, slabs, init, out_blocks, tile_size):
    rows, width = slabs[0].shape

    def whole(g, map_ref):
        return (0, 0)

    def out_map(g, map_ref):
        return (0, 0, 0)

    return pl.pallas_call(
        _combine_kernel,
        out_shape=jax.ShapeDtypeStruct((out_blocks, tile_size, width), jnp.float32),
        grid_spec=pltpu.PrefetchScalarGridSpec(
            num_scalar_prefetch=1,
            grid=(1,),
            in_specs=[pl.BlockSpec((rows, width), whole) for _ in slabs]
            + [pl.BlockSpec((out_blocks * tile_size, width), whole)],
            out_specs=pl.BlockSpec((out_blocks, tile_size, width), out_map),
        ),
        compiler_params=pltpu.CompilerParams(dimension_semantics=("arbitrary",)),
        cost_estimate=pl.CostEstimate(
            flops=len(slabs) * CAP * tile_size * width,
            transcendentals=0,
            bytes_accessed=(len(slabs) * CAP + 2 * out_blocks) * tile_size * width * 4,
        ),
    )(block_map, *slabs, init)


def _pick(stacked, index):
    return lax.dynamic_index_in_dim(stacked, index, axis=0, keepdims=False)


def shards(cotangent, preact, aggregated, weight, tile_values, tile_rows, tile_cols, tile_counts):
    node_rows, width = cotangent.shape
    tile_size = tile_values.shape[1]
    dom_count = lax.axis_size("dom")
    loop_count = lax.axis_size("loop")
    dom_index = lax.axis_index("dom")
    loop_index = lax.axis_index("loop")
    total_nodes = node_rows * dom_count * loop_count
    local_blocks = node_rows // tile_size
    tile_total = tile_rows.shape[1]

    masked = jnp.where(preact > 0, cotangent, jnp.zeros_like(cotangent))
    weight_term = jnp.dot(aggregated.T, masked, preferred_element_type=jnp.float32) * (
        1.0 / math.sqrt(total_nodes)
    )
    projected = jnp.dot(masked, weight.T, preferred_element_type=jnp.float32).astype(jnp.bfloat16)

    pieces = [projected]
    for shift in range(1, loop_count):
        pairs = [(i, (i + shift) % loop_count) for i in range(loop_count)]
        pieces.append(lax.ppermute(projected, "loop", pairs))
    partition = jnp.concatenate(pieces, axis=0).reshape(
        loop_count * local_blocks, tile_size, width
    )
    partition, weight_term = lax.optimization_barrier((partition, weight_term))
    terms = [weight_term]
    for shift in range(1, loop_count):
        pairs = [(i, (i + shift) % loop_count) for i in range(loop_count)]
        terms.append(lax.ppermute(weight_term, "loop", pairs))
    terms = jnp.stack(terms)
    loop_sum = _pick(terms, loop_index % loop_count)
    for source in range(1, loop_count):
        loop_sum = loop_sum + _pick(terms, (loop_index - source) % loop_count)

    rows = tile_rows[0]
    source_loop = rows // local_blocks
    rows = ((loop_index - source_loop) % loop_count) * local_blocks + rows % local_blocks

    cols = tile_cols[0]
    live = jnp.arange(tile_total, dtype=jnp.int32) < tile_counts[0]
    all_blocks = dom_count * local_blocks
    onehot = cols[:, None] == jnp.arange(all_blocks, dtype=jnp.int32)[None, :]
    present = jnp.any(onehot & live[:, None], axis=0).reshape(dom_count, local_blocks)
    present = present.astype(jnp.int32)
    rank = jnp.cumsum(present, axis=1) - 1
    tile_rank = jnp.sum(jnp.where(onehot, rank.reshape(1, -1), 0), axis=1)
    tile_rank = jnp.clip(tile_rank, 0, CAP - 1)
    block_ids = jnp.arange(local_blocks, dtype=jnp.int32)
    table = jnp.stack(
        [jnp.sum(jnp.where((rank == k) & (present > 0), block_ids[None, :], 0), axis=1) for k in range(CAP)],
        axis=1,
    )
    half = dom_count // 2
    side = dom_index // half
    pos = dom_index % half
    dest_dom = cols // local_blocks
    cross = (dest_dom // half != side).astype(jnp.int32)
    slots = (cross * half + (dest_dom % half - pos) % half) * CAP + tile_rank
    order = jnp.arange(dom_count, dtype=jnp.int32)
    order_side = jnp.where(order // half == 0, side, 1 - side)
    order = order_side * half + (pos + order % half) % half
    dom_ids = jnp.arange(dom_count, dtype=jnp.int32)
    rotate = order[:, None] == dom_ids[None, :]
    table = jnp.sum(jnp.where(rotate[:, :, None], table[None, :, :], 0), axis=1)

    chunk = width // dom_count
    id_rows = jnp.zeros((dom_count, 8, width), jnp.float32)
    id_rows = id_rows.at[:, 0, :CAP].set(table.astype(jnp.float32))
    extra = jnp.concatenate([id_rows, jnp.zeros((dom_count, 2 * chunk, width), jnp.float32)], axis=1)

    compact = _spmm(rows, slots, tile_counts, tile_values, partition, extra)
    body_rows = CAP * tile_size
    chunks = loop_sum.reshape(dom_count, chunk, width)
    first = jnp.stack([_pick(chunks, order[i]) for i in range(dom_count)])
    second = jnp.concatenate(
        [jnp.zeros((half, chunk, width), jnp.float32), first[:half]], axis=0
    )
    compact = lax.dynamic_update_slice(
        compact, jnp.concatenate([first, second], axis=1), (0, body_rows + 8, 0)
    )

    def within(shift):
        return [(i, (i // half) * half + (i % half + shift) % half) for i in range(dom_count)]

    swap = [(i, (1 - i // half) * half + i % half) for i in range(dom_count)]

    def ids_of(slabs):
        return jnp.concatenate([slab[body_rows, :CAP] for slab in slabs]).astype(jnp.int32)

    relay = [compact[half]]
    for shift in range(1, half):
        relay.append(lax.ppermute(compact[half + shift], "dom", within(shift)))
    lead = body_rows + 8
    relay_chunk = relay[0][lead:lead + chunk]
    own = relay[0][lead + chunk:lead + 2 * chunk]
    for slab in relay[1:]:
        relay_chunk = relay_chunk + slab[lead:lead + chunk]
        own = own + slab[lead + chunk:lead + 2 * chunk]
    own = own + lax.ppermute(relay_chunk, "dom", swap)
    zeros = jnp.zeros((local_blocks * tile_size, width), jnp.float32)
    payload = _combine(ids_of(relay), relay, zeros, local_blocks, tile_size)

    held = [own]
    for shift in range(1, half):
        held.append(lax.ppermute(own, "dom", within(shift)))
    held = jnp.stack(held)
    half_chunks = jnp.concatenate(
        [_pick(held, (pos - q) % half) for q in range(half)], axis=0
    )
    payload = jnp.concatenate([payload.reshape(node_rows, width), half_chunks], axis=0)

    direct = [compact[shift, :body_rows + 8] for shift in range(1, half)]
    direct, relay = lax.optimization_barrier((direct, relay))
    received = [compact[0, :body_rows + 8]]
    for shift in range(1, half):
        received.append(lax.ppermute(direct[shift - 1], "dom", within(shift)))
    partner = lax.ppermute(payload, "dom", swap)
    node_grad = _combine(ids_of(received), received, partner, local_blocks, tile_size)
    node_grad = node_grad.reshape(node_rows, width)
    other_chunks = partner[node_rows:]
    weight_grad = jnp.where(
        side == 0,
        jnp.concatenate([half_chunks, other_chunks], axis=0),
        jnp.concatenate([other_chunks, half_chunks], axis=0),
    )
    return (node_grad, weight_grad)


def solution(mesh):
    return jax.shard_map(
        shards,
        mesh=mesh,
        in_specs=(
            P(("dom", "loop"), None),
            P(("dom", "loop"), None),
            P(("dom", "loop"), None),
            P(),
            P(("dom", "loop"), None, None),
            P(("dom", "loop"), None),
            P(("dom", "loop"), None),
            P(("dom", "loop")),
        ),
        out_specs=(P(("dom", "loop"), None), P()),
        check_vma=False,
    )
```

```python
import math

import jax
import jax.numpy as jnp
from jax import lax
from jax.experimental import pallas as pl
from jax.experimental.pallas import tpu as pltpu
from jax.sharding import PartitionSpec as P

GROUP = 64
CAP = 4


def _spmm_kernel(rows_ref, slots_ref, cnt_ref, tv_ref, part_ref, extra_ref, out_ref):
    g = pl.program_id(0)
    count = cnt_ref[0]
    group, tile_size, _ = tv_ref.shape
    base = g * group
    body_rows = CAP * tile_size

    @pl.when(g == 0)
    def _():
        out_ref[:, :body_rows, :] = jnp.zeros(
            (out_ref.shape[0], body_rows, out_ref.shape[2]), out_ref.dtype
        )
        out_ref[:, body_rows:, :] = extra_ref[...]

    def run(masked):
        for t in range(group):
            j = base + t
            r = rows_ref[j]
            c = slots_ref[j]
            term = lax.dot_general(
                tv_ref[t],
                part_ref[r],
                (((0,), (0,)), ((), ())),
                preferred_element_type=jnp.float32,
            )
            if masked:
                term = jnp.where(j < count, term, 0.0)
            dest = c // CAP
            start = pl.multiple_of((c % CAP) * tile_size, tile_size)
            window = out_ref.at[dest, pl.ds(start, tile_size), :]
            window[...] += term

    full = base + group <= count

    @pl.when(full)
    def _():
        run(False)

    @pl.when(jnp.logical_and(base < count, jnp.logical_not(full)))
    def _():
        run(True)


def _spmm(rows, slots, count, tile_values, partition, extra):
    tiles, tile_size, _ = tile_values.shape
    part_blocks, _, width = partition.shape
    dests, extra_rows, _ = extra.shape
    out_rows = CAP * tile_size + extra_rows
    group = math.gcd(tiles, GROUP)

    def tv_map(g, rows_ref, slots_ref, cnt_ref):
        last = jnp.maximum((cnt_ref[0] + group - 1) // group - 1, 0)
        return (jnp.minimum(g, last), 0, 0)

    def whole(g, rows_ref, slots_ref, cnt_ref):
        return (0, 0, 0)

    return pl.pallas_call(
        _spmm_kernel,
        out_shape=jax.ShapeDtypeStruct((dests, out_rows, width), jnp.float32),
        grid_spec=pltpu.PrefetchScalarGridSpec(
            num_scalar_prefetch=3,
            grid=(tiles // group,),
            in_specs=[
                pl.BlockSpec((group, tile_size, tile_size), tv_map),
                pl.BlockSpec((part_blocks, tile_size, width), whole),
                pl.BlockSpec((dests, extra_rows, width), whole),
            ],
            out_specs=pl.BlockSpec((dests, out_rows, width), whole),
        ),
        compiler_params=pltpu.CompilerParams(
            dimension_semantics=("arbitrary",),
            vmem_limit_bytes=50 * 1024 * 1024,
        ),
        cost_estimate=pl.CostEstimate(
            flops=2 * tiles * tile_size * tile_size * width,
            transcendentals=0,
            bytes_accessed=tiles * tile_size * tile_size * 2 + dests * out_rows * width * 4,
        ),
    )(rows, slots, count, tile_values, partition, extra)


def _combine_kernel(map_ref, *refs):
    slab_refs = refs[:-2]
    init_ref, out_ref = refs[-2:]
    out_blocks, tile_size, width = out_ref.shape
    out_ref[...] = init_ref[...].reshape(out_blocks, tile_size, width)
    for n, slab_ref in enumerate(slab_refs):
        for k in range(CAP):
            b = map_ref[n * CAP + k]
            out_ref[b] += slab_ref[k * tile_size:(k + 1) * tile_size, :]


def _combine(block_map, slabs, init, out_blocks, tile_size):
    rows, width = slabs[0].shape

    def whole(g, map_ref):
        return (0, 0)

    def out_map(g, map_ref):
        return (0, 0, 0)

    return pl.pallas_call(
        _combine_kernel,
        out_shape=jax.ShapeDtypeStruct((out_blocks, tile_size, width), jnp.float32),
        grid_spec=pltpu.PrefetchScalarGridSpec(
            num_scalar_prefetch=1,
            grid=(1,),
            in_specs=[pl.BlockSpec((rows, width), whole) for _ in slabs]
            + [pl.BlockSpec((out_blocks * tile_size, width), whole)],
            out_specs=pl.BlockSpec((out_blocks, tile_size, width), out_map),
        ),
        compiler_params=pltpu.CompilerParams(dimension_semantics=("arbitrary",)),
        cost_estimate=pl.CostEstimate(
            flops=len(slabs) * CAP * tile_size * width,
            transcendentals=0,
            bytes_accessed=(len(slabs) * CAP + 2 * out_blocks) * tile_size * width * 4,
        ),
    )(block_map, *slabs, init)


def _pick(stacked, index):
    return lax.dynamic_index_in_dim(stacked, index, axis=0, keepdims=False)


def shards(cotangent, preact, aggregated, weight, tile_values, tile_rows, tile_cols, tile_counts):
    node_rows, width = cotangent.shape
    tile_size = tile_values.shape[1]
    dom_count = lax.axis_size("dom")
    loop_count = lax.axis_size("loop")
    dom_index = lax.axis_index("dom")
    loop_index = lax.axis_index("loop")
    total_nodes = node_rows * dom_count * loop_count
    local_blocks = node_rows // tile_size
    tile_total = tile_rows.shape[1]

    masked = jnp.where(preact > 0, cotangent, jnp.zeros_like(cotangent))
    weight_term = jnp.dot(aggregated.T, masked, preferred_element_type=jnp.float32) * (
        1.0 / math.sqrt(total_nodes)
    )
    projected = jnp.dot(masked, weight.T, preferred_element_type=jnp.float32).astype(jnp.bfloat16)

    pieces = [projected]
    for shift in range(1, loop_count):
        pairs = [(i, (i + shift) % loop_count) for i in range(loop_count)]
        pieces.append(lax.ppermute(projected, "loop", pairs))
    partition = jnp.concatenate(pieces, axis=0).reshape(
        loop_count * local_blocks, tile_size, width
    )
    partition, weight_term = lax.optimization_barrier((partition, weight_term))
    terms = [weight_term]
    for shift in range(1, loop_count):
        pairs = [(i, (i + shift) % loop_count) for i in range(loop_count)]
        terms.append(lax.ppermute(weight_term, "loop", pairs))
    terms = jnp.stack(terms)
    loop_sum = _pick(terms, loop_index % loop_count)
    for source in range(1, loop_count):
        loop_sum = loop_sum + _pick(terms, (loop_index - source) % loop_count)

    rows = tile_rows[0]
    source_loop = rows // local_blocks
    rows = ((loop_index - source_loop) % loop_count) * local_blocks + rows % local_blocks

    cols = tile_cols[0]
    live = jnp.arange(tile_total, dtype=jnp.int32) < tile_counts[0]
    all_blocks = dom_count * local_blocks
    onehot = cols[:, None] == jnp.arange(all_blocks, dtype=jnp.int32)[None, :]
    present = jnp.any(onehot & live[:, None], axis=0).reshape(dom_count, local_blocks)
    present = present.astype(jnp.int32)
    rank = jnp.cumsum(present, axis=1) - 1
    tile_rank = jnp.sum(jnp.where(onehot, rank.reshape(1, -1), 0), axis=1)
    tile_rank = jnp.clip(tile_rank, 0, CAP - 1)
    block_ids = jnp.arange(local_blocks, dtype=jnp.int32)
    table = jnp.stack(
        [jnp.sum(jnp.where((rank == k) & (present > 0), block_ids[None, :], 0), axis=1) for k in range(CAP)],
        axis=1,
    )
    half = dom_count // 2
    side = dom_index // half
    pos = dom_index % half
    dest_dom = cols // local_blocks
    cross = (dest_dom // half != side).astype(jnp.int32)
    slots = (cross * half + (dest_dom % half - pos) % half) * CAP + tile_rank
    order = jnp.arange(dom_count, dtype=jnp.int32)
    order_side = jnp.where(order // half == 0, side, 1 - side)
    order = order_side * half + (pos + order % half) % half
    dom_ids = jnp.arange(dom_count, dtype=jnp.int32)
    rotate = order[:, None] == dom_ids[None, :]
    table = jnp.sum(jnp.where(rotate[:, :, None], table[None, :, :], 0), axis=1)

    chunk = width // dom_count
    id_rows = jnp.zeros((dom_count, 8, width), jnp.float32)
    id_rows = id_rows.at[:, 0, :CAP].set(table.astype(jnp.float32))
    extra = jnp.concatenate([id_rows, jnp.zeros((dom_count, 2 * chunk, width), jnp.float32)], axis=1)

    compact = _spmm(rows, slots, tile_counts, tile_values, partition, extra)
    body_rows = CAP * tile_size
    chunks = loop_sum.reshape(dom_count, chunk, width)
    first = jnp.stack([_pick(chunks, order[i]) for i in range(dom_count)])
    second = jnp.concatenate(
        [jnp.zeros((half, chunk, width), jnp.float32), first[:half]], axis=0
    )
    compact = lax.dynamic_update_slice(
        compact, jnp.concatenate([first, second], axis=1), (0, body_rows + 8, 0)
    )

    def within(shift):
        return [(i, (i // half) * half + (i % half + shift) % half) for i in range(dom_count)]

    swap = [(i, (1 - i // half) * half + i % half) for i in range(dom_count)]

    def ids_of(slabs):
        return jnp.concatenate([slab[body_rows, :CAP] for slab in slabs]).astype(jnp.int32)

    relay = [compact[half]]
    for shift in range(1, half):
        relay.append(lax.ppermute(compact[half + shift], "dom", within(shift)))
    lead = body_rows + 8
    relay_chunk = relay[0][lead:lead + chunk]
    own = relay[0][lead + chunk:lead + 2 * chunk]
    for slab in relay[1:]:
        relay_chunk = relay_chunk + slab[lead:lead + chunk]
        own = own + slab[lead + chunk:lead + 2 * chunk]
    own = own + lax.ppermute(relay_chunk, "dom", swap)
    zeros = jnp.zeros((local_blocks * tile_size, width), jnp.float32)
    payload = _combine(ids_of(relay), relay, zeros, local_blocks, tile_size)

    held = [own]
    for shift in range(1, half):
        held.append(lax.ppermute(own, "dom", within(shift)))
    held = jnp.stack(held)
    half_chunks = jnp.concatenate(
        [_pick(held, (pos - q) % half) for q in range(half)], axis=0
    )
    payload = jnp.concatenate([payload.reshape(node_rows, width), half_chunks], axis=0)

    direct = [compact[shift, :body_rows + 8] for shift in range(1, half)]
    direct, relay = lax.optimization_barrier((direct, relay))
    received = [compact[0, :body_rows + 8]]
    for shift in range(1, half):
        received.append(lax.ppermute(direct[shift - 1], "dom", within(shift)))
    partner = lax.ppermute(payload, "dom", swap)
    node_grad = _combine(ids_of(received), received, partner, local_blocks, tile_size)
    node_grad = node_grad.reshape(node_rows, width)
    other_chunks = partner[node_rows:]
    weight_grad = jnp.where(
        side == 0,
        jnp.concatenate([half_chunks, other_chunks], axis=0),
        jnp.concatenate([other_chunks, half_chunks], axis=0),
    )
    return (node_grad, weight_grad)


def solution(mesh):
    return jax.shard_map(
        shards,
        mesh=mesh,
        in_specs=(
            P(("dom", "loop"), None),
            P(("dom", "loop"), None),
            P(("dom", "loop"), None),
            P(),
            P(("dom", "loop"), None, None),
            P(("dom", "loop"), None),
            P(("dom", "loop"), None),
            P(("dom", "loop")),
        ),
        out_specs=(P(("dom", "loop"), None), P()),
        check_vma=False,
    )
```

```python
import math

import jax
import jax.numpy as jnp
from jax import lax
from jax.experimental import pallas as pl
from jax.experimental.pallas import tpu as pltpu
from jax.sharding import PartitionSpec as P

GROUP = 64
CAP = 4


def _spmm_kernel(rows_ref, slots_ref, cnt_ref, tv_ref, part_ref, extra_ref, out_ref):
    g = pl.program_id(0)
    count = cnt_ref[0]
    group, tile_size, _ = tv_ref.shape
    base = g * group
    body_rows = CAP * tile_size

    @pl.when(g == 0)
    def _():
        out_ref[:, :body_rows, :] = jnp.zeros(
            (out_ref.shape[0], body_rows, out_ref.shape[2]), out_ref.dtype
        )
        out_ref[:, body_rows:, :] = extra_ref[...]

    def run(masked):
        for t in range(group):
            j = base + t
            r = rows_ref[j]
            c = slots_ref[j]
            term = lax.dot_general(
                tv_ref[t],
                part_ref[r],
                (((0,), (0,)), ((), ())),
                preferred_element_type=jnp.float32,
            )
            if masked:
                term = jnp.where(j < count, term, 0.0)
            dest = c // CAP
            start = pl.multiple_of((c % CAP) * tile_size, tile_size)
            window = out_ref.at[dest, pl.ds(start, tile_size), :]
            window[...] += term

    full = base + group <= count

    @pl.when(full)
    def _():
        run(False)

    @pl.when(jnp.logical_and(base < count, jnp.logical_not(full)))
    def _():
        run(True)


def _spmm(rows, slots, count, tile_values, partition, extra):
    tiles, tile_size, _ = tile_values.shape
    part_blocks, _, width = partition.shape
    dests, extra_rows, _ = extra.shape
    out_rows = CAP * tile_size + extra_rows
    group = math.gcd(tiles, GROUP)

    def tv_map(g, rows_ref, slots_ref, cnt_ref):
        last = jnp.maximum((cnt_ref[0] + group - 1) // group - 1, 0)
        return (jnp.minimum(g, last), 0, 0)

    def whole(g, rows_ref, slots_ref, cnt_ref):
        return (0, 0, 0)

    return pl.pallas_call(
        _spmm_kernel,
        out_shape=jax.ShapeDtypeStruct((dests, out_rows, width), jnp.float32),
        grid_spec=pltpu.PrefetchScalarGridSpec(
            num_scalar_prefetch=3,
            grid=(tiles // group,),
            in_specs=[
                pl.BlockSpec((group, tile_size, tile_size), tv_map),
                pl.BlockSpec((part_blocks, tile_size, width), whole),
                pl.BlockSpec((dests, extra_rows, width), whole),
            ],
            out_specs=pl.BlockSpec((dests, out_rows, width), whole),
        ),
        compiler_params=pltpu.CompilerParams(
            dimension_semantics=("arbitrary",),
            vmem_limit_bytes=50 * 1024 * 1024,
        ),
        cost_estimate=pl.CostEstimate(
            flops=2 * tiles * tile_size * tile_size * width,
            transcendentals=0,
            bytes_accessed=tiles * tile_size * tile_size * 2 + dests * out_rows * width * 4,
        ),
    )(rows, slots, count, tile_values, partition, extra)


def _combine_kernel(map_ref, *refs):
    slab_refs = refs[:-2]
    init_ref, out_ref = refs[-2:]
    out_blocks, tile_size, width = out_ref.shape
    out_ref[...] = init_ref[...].reshape(out_blocks, tile_size, width)
    for n, slab_ref in enumerate(slab_refs):
        for k in range(CAP):
            b = map_ref[n * CAP + k]
            out_ref[b] += slab_ref[k * tile_size:(k + 1) * tile_size, :]


def _combine(block_map, slabs, init, out_blocks, tile_size):
    rows, width = slabs[0].shape

    def whole(g, map_ref):
        return (0, 0)

    def out_map(g, map_ref):
        return (0, 0, 0)

    return pl.pallas_call(
        _combine_kernel,
        out_shape=jax.ShapeDtypeStruct((out_blocks, tile_size, width), jnp.float32),
        grid_spec=pltpu.PrefetchScalarGridSpec(
            num_scalar_prefetch=1,
            grid=(1,),
            in_specs=[pl.BlockSpec((rows, width), whole) for _ in slabs]
            + [pl.BlockSpec((out_blocks * tile_size, width), whole)],
            out_specs=pl.BlockSpec((out_blocks, tile_size, width), out_map),
        ),
        compiler_params=pltpu.CompilerParams(dimension_semantics=("arbitrary",)),
        cost_estimate=pl.CostEstimate(
            flops=len(slabs) * CAP * tile_size * width,
            transcendentals=0,
            bytes_accessed=(len(slabs) * CAP + 2 * out_blocks) * tile_size * width * 4,
        ),
    )(block_map, *slabs, init)


def _pick(stacked, index):
    return lax.dynamic_index_in_dim(stacked, index, axis=0, keepdims=False)


def shards(cotangent, preact, aggregated, weight, tile_values, tile_rows, tile_cols, tile_counts):
    node_rows, width = cotangent.shape
    tile_size = tile_values.shape[1]
    dom_count = lax.axis_size("dom")
    loop_count = lax.axis_size("loop")
    dom_index = lax.axis_index("dom")
    loop_index = lax.axis_index("loop")
    total_nodes = node_rows * dom_count * loop_count
    local_blocks = node_rows // tile_size
    tile_total = tile_rows.shape[1]

    masked = jnp.where(preact > 0, cotangent, jnp.zeros_like(cotangent))
    weight_term = jnp.dot(aggregated.T, masked, preferred_element_type=jnp.float32) * (
        1.0 / math.sqrt(total_nodes)
    )
    projected = jnp.dot(masked, weight.T, preferred_element_type=jnp.float32).astype(jnp.bfloat16)

    pieces = [projected]
    for shift in range(1, loop_count):
        pairs = [(i, (i + shift) % loop_count) for i in range(loop_count)]
        pieces.append(lax.ppermute(projected, "loop", pairs))
    partition = jnp.concatenate(pieces, axis=0).reshape(
        loop_count * local_blocks, tile_size, width
    )
    step = 1
    while step < dom_count:
        pairs = [(i, i ^ step) for i in range(dom_count)]
        weight_term = weight_term + lax.ppermute(weight_term, "dom", pairs)
        step *= 2
    terms = [weight_term]
    for shift in range(1, loop_count):
        pairs = [(i, (i + shift) % loop_count) for i in range(loop_count)]
        terms.append(lax.ppermute(weight_term, "loop", pairs))
    terms = jnp.stack(terms)
    weight_grad = _pick(terms, loop_index % loop_count)
    for source in range(1, loop_count):
        weight_grad = weight_grad + _pick(terms, (loop_index - source) % loop_count)

    rows = tile_rows[0]
    source_loop = rows // local_blocks
    rows = ((loop_index - source_loop) % loop_count) * local_blocks + rows % local_blocks

    cols = tile_cols[0]
    live = jnp.arange(tile_total, dtype=jnp.int32) < tile_counts[0]
    all_blocks = dom_count * local_blocks
    onehot = cols[:, None] == jnp.arange(all_blocks, dtype=jnp.int32)[None, :]
    present = jnp.any(onehot & live[:, None], axis=0).reshape(dom_count, local_blocks)
    present = present.astype(jnp.int32)
    rank = jnp.cumsum(present, axis=1) - 1
    tile_rank = jnp.sum(jnp.where(onehot, rank.reshape(1, -1), 0), axis=1)
    tile_rank = jnp.clip(tile_rank, 0, CAP - 1)
    block_ids = jnp.arange(local_blocks, dtype=jnp.int32)
    table = jnp.stack(
        [jnp.sum(jnp.where((rank == k) & (present > 0), block_ids[None, :], 0), axis=1) for k in range(CAP)],
        axis=1,
    )
    half = dom_count // 2
    side = dom_index // half
    pos = dom_index % half
    dest_dom = cols // local_blocks
    cross = (dest_dom // half != side).astype(jnp.int32)
    slots = (cross * half + (dest_dom % half - pos) % half) * CAP + tile_rank
    order = jnp.arange(dom_count, dtype=jnp.int32)
    order_side = jnp.where(order // half == 0, side, 1 - side)
    order = order_side * half + (pos + order % half) % half
    dom_ids = jnp.arange(dom_count, dtype=jnp.int32)
    rotate = order[:, None] == dom_ids[None, :]
    table = jnp.sum(jnp.where(rotate[:, :, None], table[None, :, :], 0), axis=1)

    id_rows = jnp.zeros((dom_count, 8, width), jnp.float32)
    extra = id_rows.at[:, 0, :CAP].set(table.astype(jnp.float32))

    compact = _spmm(rows, slots, tile_counts, tile_values, partition, extra)
    body_rows = CAP * tile_size

    def within(shift):
        return [(i, (i // half) * half + (i % half + shift) % half) for i in range(dom_count)]

    swap = [(i, (1 - i // half) * half + i % half) for i in range(dom_count)]

    def ids_of(slabs):
        return jnp.concatenate([slab[body_rows, :CAP] for slab in slabs]).astype(jnp.int32)

    relay = [compact[half]]
    for shift in range(1, half):
        relay.append(lax.ppermute(compact[half + shift], "dom", within(shift)))
    zeros = jnp.zeros((local_blocks * tile_size, width), jnp.float32)
    payload = _combine(ids_of(relay), relay, zeros, local_blocks, tile_size)

    direct = [compact[shift] for shift in range(1, half)]
    direct, relay = lax.optimization_barrier((direct, relay))
    received = [compact[0]]
    for shift in range(1, half):
        received.append(lax.ppermute(direct[shift - 1], "dom", within(shift)))
    partner = lax.ppermute(payload.reshape(node_rows, width), "dom", swap)
    node_grad = _combine(ids_of(received), received, partner, local_blocks, tile_size)
    node_grad = node_grad.reshape(node_rows, width)
    return (node_grad, weight_grad)


def solution(mesh):
    return jax.shard_map(
        shards,
        mesh=mesh,
        in_specs=(
            P(("dom", "loop"), None),
            P(("dom", "loop"), None),
            P(("dom", "loop"), None),
            P(),
            P(("dom", "loop"), None, None),
            P(("dom", "loop"), None),
            P(("dom", "loop"), None),
            P(("dom", "loop")),
        ),
        out_specs=(P(("dom", "loop"), None), P()),
        check_vma=False,
    )
```

```python
import math

import jax
import jax.numpy as jnp
from jax import lax
from jax.experimental import pallas as pl
from jax.experimental.pallas import tpu as pltpu
from jax.sharding import PartitionSpec as P

GROUP = 64
CAP = 4


def _spmm_kernel(rows_ref, slots_ref, cnt_ref, tv_ref, part_ref, extra_ref, out_ref):
    g = pl.program_id(0)
    count = cnt_ref[0]
    group, tile_size, _ = tv_ref.shape
    base = g * group
    body_rows = CAP * tile_size

    @pl.when(g == 0)
    def _():
        out_ref[:, :body_rows, :] = jnp.zeros(
            (out_ref.shape[0], body_rows, out_ref.shape[2]), out_ref.dtype
        )
        out_ref[:, body_rows:, :] = extra_ref[...]

    def run(masked):
        for t in range(group):
            j = base + t
            r = rows_ref[j]
            c = slots_ref[j]
            term = lax.dot_general(
                tv_ref[t],
                part_ref[r],
                (((0,), (0,)), ((), ())),
                preferred_element_type=jnp.float32,
            )
            if masked:
                term = jnp.where(j < count, term, 0.0)
            dest = c // CAP
            start = pl.multiple_of((c % CAP) * tile_size, tile_size)
            window = out_ref.at[dest, pl.ds(start, tile_size), :]
            window[...] += term

    full = base + group <= count

    @pl.when(full)
    def _():
        run(False)

    @pl.when(jnp.logical_and(base < count, jnp.logical_not(full)))
    def _():
        run(True)


def _spmm(rows, slots, count, tile_values, partition, extra):
    tiles, tile_size, _ = tile_values.shape
    part_blocks, _, width = partition.shape
    dests, extra_rows, _ = extra.shape
    out_rows = CAP * tile_size + extra_rows
    group = math.gcd(tiles, GROUP)

    def tv_map(g, rows_ref, slots_ref, cnt_ref):
        last = jnp.maximum((cnt_ref[0] + group - 1) // group - 1, 0)
        return (jnp.minimum(g, last), 0, 0)

    def whole(g, rows_ref, slots_ref, cnt_ref):
        return (0, 0, 0)

    return pl.pallas_call(
        _spmm_kernel,
        out_shape=jax.ShapeDtypeStruct((dests, out_rows, width), jnp.float32),
        grid_spec=pltpu.PrefetchScalarGridSpec(
            num_scalar_prefetch=3,
            grid=(tiles // group,),
            in_specs=[
                pl.BlockSpec((group, tile_size, tile_size), tv_map),
                pl.BlockSpec((part_blocks, tile_size, width), whole),
                pl.BlockSpec((dests, extra_rows, width), whole),
            ],
            out_specs=pl.BlockSpec((dests, out_rows, width), whole),
        ),
        compiler_params=pltpu.CompilerParams(
            dimension_semantics=("arbitrary",),
            vmem_limit_bytes=50 * 1024 * 1024,
        ),
        cost_estimate=pl.CostEstimate(
            flops=2 * tiles * tile_size * tile_size * width,
            transcendentals=0,
            bytes_accessed=tiles * tile_size * tile_size * 2 + dests * out_rows * width * 4,
        ),
    )(rows, slots, count, tile_values, partition, extra)


def _combine_kernel(map_ref, *refs):
    slab_refs = refs[:-2]
    init_ref, out_ref = refs[-2:]
    out_blocks, tile_size, width = out_ref.shape
    out_ref[...] = init_ref[...].reshape(out_blocks, tile_size, width)
    for n, slab_ref in enumerate(slab_refs):
        for k in range(CAP):
            b = map_ref[n * CAP + k]
            out_ref[b] += slab_ref[k * tile_size:(k + 1) * tile_size, :]


def _combine(block_map, slabs, init, out_blocks, tile_size):
    rows, width = slabs[0].shape

    def whole(g, map_ref):
        return (0, 0)

    def out_map(g, map_ref):
        return (0, 0, 0)

    return pl.pallas_call(
        _combine_kernel,
        out_shape=jax.ShapeDtypeStruct((out_blocks, tile_size, width), jnp.float32),
        grid_spec=pltpu.PrefetchScalarGridSpec(
            num_scalar_prefetch=1,
            grid=(1,),
            in_specs=[pl.BlockSpec((rows, width), whole) for _ in slabs]
            + [pl.BlockSpec((out_blocks * tile_size, width), whole)],
            out_specs=pl.BlockSpec((out_blocks, tile_size, width), out_map),
        ),
        compiler_params=pltpu.CompilerParams(dimension_semantics=("arbitrary",)),
        cost_estimate=pl.CostEstimate(
            flops=len(slabs) * CAP * tile_size * width,
            transcendentals=0,
            bytes_accessed=(len(slabs) * CAP + 2 * out_blocks) * tile_size * width * 4,
        ),
    )(block_map, *slabs, init)


def _pick(stacked, index):
    return lax.dynamic_index_in_dim(stacked, index, axis=0, keepdims=False)


def shards(cotangent, preact, aggregated, weight, tile_values, tile_rows, tile_cols, tile_counts):
    node_rows, width = cotangent.shape
    tile_size = tile_values.shape[1]
    dom_count = lax.axis_size("dom")
    loop_count = lax.axis_size("loop")
    dom_index = lax.axis_index("dom")
    loop_index = lax.axis_index("loop")
    total_nodes = node_rows * dom_count * loop_count
    local_blocks = node_rows // tile_size
    tile_total = tile_rows.shape[1]

    masked = jnp.where(preact > 0, cotangent, jnp.zeros_like(cotangent))
    weight_term = jnp.dot(aggregated.T, masked, preferred_element_type=jnp.float32) * (
        1.0 / math.sqrt(total_nodes)
    )
    projected = jnp.dot(masked, weight.T, preferred_element_type=jnp.float32).astype(jnp.bfloat16)

    pieces = [projected]
    for shift in range(1, loop_count):
        pairs = [(i, (i + shift) % loop_count) for i in range(loop_count)]
        pieces.append(lax.ppermute(projected, "loop", pairs))
    partition = jnp.concatenate(pieces, axis=0).reshape(
        loop_count * local_blocks, tile_size, width
    )
    step = 1
    while step < dom_count:
        pairs = [(i, i ^ step) for i in range(dom_count)]
        weight_term = weight_term + lax.ppermute(weight_term, "dom", pairs)
        step *= 2
    partition, weight_term = lax.optimization_barrier((partition, weight_term))
    terms = [weight_term]
    for shift in range(1, loop_count):
        pairs = [(i, (i + shift) % loop_count) for i in range(loop_count)]
        terms.append(lax.ppermute(weight_term, "loop", pairs))
    terms = jnp.stack(terms)
    weight_grad = _pick(terms, loop_index % loop_count)
    for source in range(1, loop_count):
        weight_grad = weight_grad + _pick(terms, (loop_index - source) % loop_count)

    rows = tile_rows[0]
    source_loop = rows // local_blocks
    rows = ((loop_index - source_loop) % loop_count) * local_blocks + rows % local_blocks

    cols = tile_cols[0]
    live = jnp.arange(tile_total, dtype=jnp.int32) < tile_counts[0]
    all_blocks = dom_count * local_blocks
    onehot = cols[:, None] == jnp.arange(all_blocks, dtype=jnp.int32)[None, :]
    present = jnp.any(onehot & live[:, None], axis=0).reshape(dom_count, local_blocks)
    present = present.astype(jnp.int32)
    rank = jnp.cumsum(present, axis=1) - 1
    tile_rank = jnp.sum(jnp.where(onehot, rank.reshape(1, -1), 0), axis=1)
    tile_rank = jnp.clip(tile_rank, 0, CAP - 1)
    block_ids = jnp.arange(local_blocks, dtype=jnp.int32)
    table = jnp.stack(
        [jnp.sum(jnp.where((rank == k) & (present > 0), block_ids[None, :], 0), axis=1) for k in range(CAP)],
        axis=1,
    )
    half = dom_count // 2
    side = dom_index // half
    pos = dom_index % half
    dest_dom = cols // local_blocks
    cross = (dest_dom // half != side).astype(jnp.int32)
    slots = (cross * half + (dest_dom % half - pos) % half) * CAP + tile_rank
    order = jnp.arange(dom_count, dtype=jnp.int32)
    order_side = jnp.where(order // half == 0, side, 1 - side)
    order = order_side * half + (pos + order % half) % half
    dom_ids = jnp.arange(dom_count, dtype=jnp.int32)
    rotate = order[:, None] == dom_ids[None, :]
    table = jnp.sum(jnp.where(rotate[:, :, None], table[None, :, :], 0), axis=1)

    id_rows = jnp.zeros((dom_count, 8, width), jnp.float32)
    extra = id_rows.at[:, 0, :CAP].set(table.astype(jnp.float32))

    compact = _spmm(rows, slots, tile_counts, tile_values, partition, extra)
    body_rows = CAP * tile_size

    def within(shift):
        return [(i, (i // half) * half + (i % half + shift) % half) for i in range(dom_count)]

    swap = [(i, (1 - i // half) * half + i % half) for i in range(dom_count)]

    def ids_of(slabs):
        return jnp.concatenate([slab[body_rows, :CAP] for slab in slabs]).astype(jnp.int32)

    relay = [compact[half]]
    for shift in range(1, half):
        relay.append(lax.ppermute(compact[half + shift], "dom", within(shift)))
    zeros = jnp.zeros((local_blocks * tile_size, width), jnp.float32)
    payload = _combine(ids_of(relay), relay, zeros, local_blocks, tile_size)

    direct = [compact[shift] for shift in range(1, half)]
    direct, relay = lax.optimization_barrier((direct, relay))
    received = [compact[0]]
    for shift in range(1, half):
        received.append(lax.ppermute(direct[shift - 1], "dom", within(shift)))
    partner = lax.ppermute(payload.reshape(node_rows, width), "dom", swap)
    node_grad = _combine(ids_of(received), received, partner, local_blocks, tile_size)
    node_grad = node_grad.reshape(node_rows, width)
    return (node_grad, weight_grad)


def solution(mesh):
    return jax.shard_map(
        shards,
        mesh=mesh,
        in_specs=(
            P(("dom", "loop"), None),
            P(("dom", "loop"), None),
            P(("dom", "loop"), None),
            P(),
            P(("dom", "loop"), None, None),
            P(("dom", "loop"), None),
            P(("dom", "loop"), None),
            P(("dom", "loop")),
        ),
        out_specs=(P(("dom", "loop"), None), P()),
        check_vma=False,
    )
```

```python
import math

import jax
import jax.numpy as jnp
from jax import lax
from jax.experimental import pallas as pl
from jax.experimental.pallas import tpu as pltpu
from jax.sharding import PartitionSpec as P

GROUP = 128
CAP = 4


def _spmm_kernel(rows_ref, slots_ref, cnt_ref, tv_ref, part_ref, extra_ref, out_ref):
    g = pl.program_id(0)
    count = cnt_ref[0]
    group, tile_size, _ = tv_ref.shape
    base = g * group
    body_rows = CAP * tile_size

    @pl.when(g == 0)
    def _():
        out_ref[:, :body_rows, :] = jnp.zeros(
            (out_ref.shape[0], body_rows, out_ref.shape[2]), out_ref.dtype
        )
        out_ref[:, body_rows:, :] = extra_ref[...]

    def run(masked):
        for t in range(group):
            j = base + t
            r = rows_ref[j]
            c = slots_ref[j]
            term = lax.dot_general(
                tv_ref[t],
                part_ref[r],
                (((0,), (0,)), ((), ())),
                preferred_element_type=jnp.float32,
            )
            if masked:
                term = jnp.where(j < count, term, 0.0)
            dest = c // CAP
            start = pl.multiple_of((c % CAP) * tile_size, tile_size)
            window = out_ref.at[dest, pl.ds(start, tile_size), :]
            window[...] += term

    full = base + group <= count

    @pl.when(full)
    def _():
        run(False)

    @pl.when(jnp.logical_and(base < count, jnp.logical_not(full)))
    def _():
        run(True)


def _spmm(rows, slots, count, tile_values, partition, extra):
    tiles, tile_size, _ = tile_values.shape
    part_blocks, _, width = partition.shape
    dests, extra_rows, _ = extra.shape
    out_rows = CAP * tile_size + extra_rows
    group = math.gcd(tiles, GROUP)

    def tv_map(g, rows_ref, slots_ref, cnt_ref):
        last = jnp.maximum((cnt_ref[0] + group - 1) // group - 1, 0)
        return (jnp.minimum(g, last), 0, 0)

    def whole(g, rows_ref, slots_ref, cnt_ref):
        return (0, 0, 0)

    return pl.pallas_call(
        _spmm_kernel,
        out_shape=jax.ShapeDtypeStruct((dests, out_rows, width), jnp.float32),
        grid_spec=pltpu.PrefetchScalarGridSpec(
            num_scalar_prefetch=3,
            grid=(tiles // group,),
            in_specs=[
                pl.BlockSpec((group, tile_size, tile_size), tv_map),
                pl.BlockSpec((part_blocks, tile_size, width), whole),
                pl.BlockSpec((dests, extra_rows, width), whole),
            ],
            out_specs=pl.BlockSpec((dests, out_rows, width), whole),
        ),
        compiler_params=pltpu.CompilerParams(
            dimension_semantics=("arbitrary",),
            vmem_limit_bytes=50 * 1024 * 1024,
        ),
        cost_estimate=pl.CostEstimate(
            flops=2 * tiles * tile_size * tile_size * width,
            transcendentals=0,
            bytes_accessed=tiles * tile_size * tile_size * 2 + dests * out_rows * width * 4,
        ),
    )(rows, slots, count, tile_values, partition, extra)


def _combine_kernel(map_ref, *refs):
    slab_refs = refs[:-2]
    init_ref, out_ref = refs[-2:]
    out_blocks, tile_size, width = out_ref.shape
    out_ref[...] = init_ref[...].reshape(out_blocks, tile_size, width)
    for n, slab_ref in enumerate(slab_refs):
        for k in range(CAP):
            b = map_ref[n * CAP + k]
            out_ref[b] += slab_ref[k * tile_size:(k + 1) * tile_size, :]


def _combine(block_map, slabs, init, out_blocks, tile_size):
    rows, width = slabs[0].shape

    def whole(g, map_ref):
        return (0, 0)

    def out_map(g, map_ref):
        return (0, 0, 0)

    return pl.pallas_call(
        _combine_kernel,
        out_shape=jax.ShapeDtypeStruct((out_blocks, tile_size, width), jnp.float32),
        grid_spec=pltpu.PrefetchScalarGridSpec(
            num_scalar_prefetch=1,
            grid=(1,),
            in_specs=[pl.BlockSpec((rows, width), whole) for _ in slabs]
            + [pl.BlockSpec((out_blocks * tile_size, width), whole)],
            out_specs=pl.BlockSpec((out_blocks, tile_size, width), out_map),
        ),
        compiler_params=pltpu.CompilerParams(dimension_semantics=("arbitrary",)),
        cost_estimate=pl.CostEstimate(
            flops=len(slabs) * CAP * tile_size * width,
            transcendentals=0,
            bytes_accessed=(len(slabs) * CAP + 2 * out_blocks) * tile_size * width * 4,
        ),
    )(block_map, *slabs, init)


def _pick(stacked, index):
    return lax.dynamic_index_in_dim(stacked, index, axis=0, keepdims=False)


def shards(cotangent, preact, aggregated, weight, tile_values, tile_rows, tile_cols, tile_counts):
    node_rows, width = cotangent.shape
    tile_size = tile_values.shape[1]
    dom_count = lax.axis_size("dom")
    loop_count = lax.axis_size("loop")
    dom_index = lax.axis_index("dom")
    loop_index = lax.axis_index("loop")
    total_nodes = node_rows * dom_count * loop_count
    local_blocks = node_rows // tile_size
    tile_total = tile_rows.shape[1]

    masked = jnp.where(preact > 0, cotangent, jnp.zeros_like(cotangent))
    weight_term = jnp.dot(aggregated.T, masked, preferred_element_type=jnp.float32) * (
        1.0 / math.sqrt(total_nodes)
    )
    projected = jnp.dot(masked, weight.T, preferred_element_type=jnp.float32).astype(jnp.bfloat16)

    pieces = [projected]
    for shift in range(1, loop_count):
        pairs = [(i, (i + shift) % loop_count) for i in range(loop_count)]
        pieces.append(lax.ppermute(projected, "loop", pairs))
    partition = jnp.concatenate(pieces, axis=0).reshape(
        loop_count * local_blocks, tile_size, width
    )
    step = 1
    while step < dom_count:
        pairs = [(i, i ^ step) for i in range(dom_count)]
        weight_term = weight_term + lax.ppermute(weight_term, "dom", pairs)
        step *= 2
    partition, weight_term = lax.optimization_barrier((partition, weight_term))
    terms = [weight_term]
    for shift in range(1, loop_count):
        pairs = [(i, (i + shift) % loop_count) for i in range(loop_count)]
        terms.append(lax.ppermute(weight_term, "loop", pairs))
    terms = jnp.stack(terms)
    weight_grad = _pick(terms, loop_index % loop_count)
    for source in range(1, loop_count):
        weight_grad = weight_grad + _pick(terms, (loop_index - source) % loop_count)

    rows = tile_rows[0]
    source_loop = rows // local_blocks
    rows = ((loop_index - source_loop) % loop_count) * local_blocks + rows % local_blocks

    cols = tile_cols[0]
    live = jnp.arange(tile_total, dtype=jnp.int32) < tile_counts[0]
    all_blocks = dom_count * local_blocks
    onehot = cols[:, None] == jnp.arange(all_blocks, dtype=jnp.int32)[None, :]
    present = jnp.any(onehot & live[:, None], axis=0).reshape(dom_count, local_blocks)
    present = present.astype(jnp.int32)
    rank = jnp.cumsum(present, axis=1) - 1
    tile_rank = jnp.sum(jnp.where(onehot, rank.reshape(1, -1), 0), axis=1)
    tile_rank = jnp.clip(tile_rank, 0, CAP - 1)
    block_ids = jnp.arange(local_blocks, dtype=jnp.int32)
    table = jnp.stack(
        [jnp.sum(jnp.where((rank == k) & (present > 0), block_ids[None, :], 0), axis=1) for k in range(CAP)],
        axis=1,
    )
    half = dom_count // 2
    side = dom_index // half
    pos = dom_index % half
    dest_dom = cols // local_blocks
    cross = (dest_dom // half != side).astype(jnp.int32)
    slots = (cross * half + (dest_dom % half - pos) % half) * CAP + tile_rank
    order = jnp.arange(dom_count, dtype=jnp.int32)
    order_side = jnp.where(order // half == 0, side, 1 - side)
    order = order_side * half + (pos + order % half) % half
    dom_ids = jnp.arange(dom_count, dtype=jnp.int32)
    rotate = order[:, None] == dom_ids[None, :]
    table = jnp.sum(jnp.where(rotate[:, :, None], table[None, :, :], 0), axis=1)

    id_rows = jnp.zeros((dom_count, 8, width), jnp.float32)
    extra = id_rows.at[:, 0, :CAP].set(table.astype(jnp.float32))

    compact = _spmm(rows, slots, tile_counts, tile_values, partition, extra)
    body_rows = CAP * tile_size

    def within(shift):
        return [(i, (i // half) * half + (i % half + shift) % half) for i in range(dom_count)]

    swap = [(i, (1 - i // half) * half + i % half) for i in range(dom_count)]

    def ids_of(slabs):
        return jnp.concatenate([slab[body_rows, :CAP] for slab in slabs]).astype(jnp.int32)

    relay = [compact[half]]
    for shift in range(1, half):
        relay.append(lax.ppermute(compact[half + shift], "dom", within(shift)))
    zeros = jnp.zeros((local_blocks * tile_size, width), jnp.float32)
    payload = _combine(ids_of(relay), relay, zeros, local_blocks, tile_size)

    direct = [compact[shift] for shift in range(1, half)]
    direct, relay = lax.optimization_barrier((direct, relay))
    received = [compact[0]]
    for shift in range(1, half):
        received.append(lax.ppermute(direct[shift - 1], "dom", within(shift)))
    partner = lax.ppermute(payload.reshape(node_rows, width), "dom", swap)
    node_grad = _combine(ids_of(received), received, partner, local_blocks, tile_size)
    node_grad = node_grad.reshape(node_rows, width)
    return (node_grad, weight_grad)


def solution(mesh):
    return jax.shard_map(
        shards,
        mesh=mesh,
        in_specs=(
            P(("dom", "loop"), None),
            P(("dom", "loop"), None),
            P(("dom", "loop"), None),
            P(),
            P(("dom", "loop"), None, None),
            P(("dom", "loop"), None),
            P(("dom", "loop"), None),
            P(("dom", "loop")),
        ),
        out_specs=(P(("dom", "loop"), None), P()),
        check_vma=False,
    )
```

```python
import functools
import math

import jax
import jax.numpy as jnp
from jax import lax
from jax.experimental import pallas as pl
from jax.experimental.pallas import tpu as pltpu
from jax.sharding import PartitionSpec as P

GROUP = 128
CAP = 4


def _spmm_kernel(rows_ref, slots_ref, cnt_ref, tv_ref, part_ref, extra_ref, out_ref):
    g = pl.program_id(0)
    count = cnt_ref[0]
    group, tile_size, _ = tv_ref.shape
    base = g * group
    body_rows = CAP * tile_size

    @pl.when(g == 0)
    def _():
        out_ref[:, :body_rows, :] = jnp.zeros(
            (out_ref.shape[0], body_rows, out_ref.shape[2]), out_ref.dtype
        )
        out_ref[:, body_rows:, :] = extra_ref[...]

    def run(masked):
        for t in range(group):
            j = base + t
            r = rows_ref[j]
            c = slots_ref[j]
            term = lax.dot_general(
                tv_ref[t],
                part_ref[r],
                (((0,), (0,)), ((), ())),
                preferred_element_type=jnp.float32,
            )
            if masked:
                term = jnp.where(j < count, term, 0.0)
            dest = c // CAP
            start = pl.multiple_of((c % CAP) * tile_size, tile_size)
            window = out_ref.at[dest, pl.ds(start, tile_size), :]
            window[...] += term

    full = base + group <= count

    @pl.when(full)
    def _():
        run(False)

    @pl.when(jnp.logical_and(base < count, jnp.logical_not(full)))
    def _():
        run(True)


def _spmm(rows, slots, count, tile_values, partition, extra):
    tiles, tile_size, _ = tile_values.shape
    part_blocks, _, width = partition.shape
    dests, extra_rows, _ = extra.shape
    out_rows = CAP * tile_size + extra_rows
    group = math.gcd(tiles, GROUP)

    def tv_map(g, rows_ref, slots_ref, cnt_ref):
        last = jnp.maximum((cnt_ref[0] + group - 1) // group - 1, 0)
        return (jnp.minimum(g, last), 0, 0)

    def whole(g, rows_ref, slots_ref, cnt_ref):
        return (0, 0, 0)

    return pl.pallas_call(
        _spmm_kernel,
        out_shape=jax.ShapeDtypeStruct((dests, out_rows, width), jnp.float32),
        grid_spec=pltpu.PrefetchScalarGridSpec(
            num_scalar_prefetch=3,
            grid=(tiles // group,),
            in_specs=[
                pl.BlockSpec((group, tile_size, tile_size), tv_map),
                pl.BlockSpec((part_blocks, tile_size, width), whole),
                pl.BlockSpec((dests, extra_rows, width), whole),
            ],
            out_specs=pl.BlockSpec((dests, out_rows, width), whole),
        ),
        compiler_params=pltpu.CompilerParams(
            dimension_semantics=("arbitrary",),
            vmem_limit_bytes=50 * 1024 * 1024,
        ),
        cost_estimate=pl.CostEstimate(
            flops=2 * tiles * tile_size * tile_size * width,
            transcendentals=0,
            bytes_accessed=tiles * tile_size * tile_size * 2 + dests * out_rows * width * 4,
        ),
    )(rows, slots, count, tile_values, partition, extra)


def _combine_kernel(map_ref, *refs, has_init):
    out_ref = refs[-1]
    out_blocks, tile_size, width = out_ref.shape
    if has_init:
        slab_refs = refs[:-2]
        out_ref[...] = refs[-2][...].reshape(out_blocks, tile_size, width)
    else:
        slab_refs = refs[:-1]
        out_ref[...] = jnp.zeros(out_ref.shape, out_ref.dtype)
    for n, slab_ref in enumerate(slab_refs):
        for k in range(CAP):
            b = map_ref[n * CAP + k]
            out_ref[b] += slab_ref[k * tile_size:(k + 1) * tile_size, :]


def _combine(block_map, slabs, init, out_blocks, tile_size):
    rows, width = slabs[0].shape

    def whole(g, map_ref):
        return (0, 0)

    def out_map(g, map_ref):
        return (0, 0, 0)

    has_init = init is not None
    init_args = (init,) if has_init else ()
    return pl.pallas_call(
        functools.partial(_combine_kernel, has_init=has_init),
        out_shape=jax.ShapeDtypeStruct((out_blocks, tile_size, width), jnp.float32),
        grid_spec=pltpu.PrefetchScalarGridSpec(
            num_scalar_prefetch=1,
            grid=(1,),
            in_specs=[pl.BlockSpec((rows, width), whole) for _ in slabs]
            + [pl.BlockSpec((out_blocks * tile_size, width), whole) for _ in init_args],
            out_specs=pl.BlockSpec((out_blocks, tile_size, width), out_map),
        ),
        compiler_params=pltpu.CompilerParams(dimension_semantics=("arbitrary",)),
        cost_estimate=pl.CostEstimate(
            flops=len(slabs) * CAP * tile_size * width,
            transcendentals=0,
            bytes_accessed=(len(slabs) * CAP + 2 * out_blocks) * tile_size * width * 4,
        ),
    )(block_map, *slabs, *init_args)


def _pick(stacked, index):
    return lax.dynamic_index_in_dim(stacked, index, axis=0, keepdims=False)


def shards(cotangent, preact, aggregated, weight, tile_values, tile_rows, tile_cols, tile_counts):
    node_rows, width = cotangent.shape
    tile_size = tile_values.shape[1]
    dom_count = lax.axis_size("dom")
    loop_count = lax.axis_size("loop")
    dom_index = lax.axis_index("dom")
    loop_index = lax.axis_index("loop")
    total_nodes = node_rows * dom_count * loop_count
    local_blocks = node_rows // tile_size
    tile_total = tile_rows.shape[1]

    masked = jnp.where(preact > 0, cotangent, jnp.zeros_like(cotangent))
    weight_term = jnp.dot(aggregated.T, masked, preferred_element_type=jnp.float32) * (
        1.0 / math.sqrt(total_nodes)
    )
    projected = jnp.dot(masked, weight.T, preferred_element_type=jnp.float32).astype(jnp.bfloat16)

    pieces = [projected]
    for shift in range(1, loop_count):
        pairs = [(i, (i + shift) % loop_count) for i in range(loop_count)]
        pieces.append(lax.ppermute(projected, "loop", pairs))
    partition = jnp.concatenate(pieces, axis=0).reshape(
        loop_count * local_blocks, tile_size, width
    )
    step = 1
    while step < dom_count:
        pairs = [(i, i ^ step) for i in range(dom_count)]
        weight_term = weight_term + lax.ppermute(weight_term, "dom", pairs)
        step *= 2
    partition, weight_term = lax.optimization_barrier((partition, weight_term))
    terms = [weight_term]
    for shift in range(1, loop_count):
        pairs = [(i, (i + shift) % loop_count) for i in range(loop_count)]
        terms.append(lax.ppermute(weight_term, "loop", pairs))
    terms = jnp.stack(terms)
    weight_grad = _pick(terms, loop_index % loop_count)
    for source in range(1, loop_count):
        weight_grad = weight_grad + _pick(terms, (loop_index - source) % loop_count)

    rows = tile_rows[0]
    source_loop = rows // local_blocks
    rows = ((loop_index - source_loop) % loop_count) * local_blocks + rows % local_blocks

    cols = tile_cols[0]
    live = jnp.arange(tile_total, dtype=jnp.int32) < tile_counts[0]
    all_blocks = dom_count * local_blocks
    onehot = cols[:, None] == jnp.arange(all_blocks, dtype=jnp.int32)[None, :]
    present = jnp.any(onehot & live[:, None], axis=0).reshape(dom_count, local_blocks)
    present = present.astype(jnp.int32)
    rank = jnp.cumsum(present, axis=1) - 1
    tile_rank = jnp.sum(jnp.where(onehot, rank.reshape(1, -1), 0), axis=1)
    tile_rank = jnp.clip(tile_rank, 0, CAP - 1)
    block_ids = jnp.arange(local_blocks, dtype=jnp.int32)
    table = jnp.stack(
        [jnp.sum(jnp.where((rank == k) & (present > 0), block_ids[None, :], 0), axis=1) for k in range(CAP)],
        axis=1,
    )
    half = dom_count // 2
    side = dom_index // half
    pos = dom_index % half
    dest_dom = cols // local_blocks
    cross = (dest_dom // half != side).astype(jnp.int32)
    slots = (cross * half + (dest_dom % half - pos) % half) * CAP + tile_rank
    order = jnp.arange(dom_count, dtype=jnp.int32)
    order_side = jnp.where(order // half == 0, side, 1 - side)
    order = order_side * half + (pos + order % half) % half
    dom_ids = jnp.arange(dom_count, dtype=jnp.int32)
    rotate = order[:, None] == dom_ids[None, :]
    table = jnp.sum(jnp.where(rotate[:, :, None], table[None, :, :], 0), axis=1)

    id_rows = jnp.zeros((dom_count, 8, width), jnp.float32)
    extra = id_rows.at[:, 0, :CAP].set(table.astype(jnp.float32))

    compact = _spmm(rows, slots, tile_counts, tile_values, partition, extra)
    body_rows = CAP * tile_size

    def within(shift):
        return [(i, (i // half) * half + (i % half + shift) % half) for i in range(dom_count)]

    swap = [(i, (1 - i // half) * half + i % half) for i in range(dom_count)]

    def ids_of(slabs):
        return jnp.concatenate([slab[body_rows, :CAP] for slab in slabs]).astype(jnp.int32)

    relay = [compact[half]]
    for shift in range(1, half):
        relay.append(lax.ppermute(compact[half + shift], "dom", within(shift)))
    payload = _combine(ids_of(relay), relay, None, local_blocks, tile_size)

    direct = [compact[shift] for shift in range(1, half)]
    direct, relay = lax.optimization_barrier((direct, relay))
    received = [compact[0]]
    for shift in range(1, half):
        received.append(lax.ppermute(direct[shift - 1], "dom", within(shift)))
    partner = lax.ppermute(payload.reshape(node_rows, width), "dom", swap)
    node_grad = _combine(ids_of(received), received, partner, local_blocks, tile_size)
    node_grad = node_grad.reshape(node_rows, width)
    return (node_grad, weight_grad)


def solution(mesh):
    return jax.shard_map(
        shards,
        mesh=mesh,
        in_specs=(
            P(("dom", "loop"), None),
            P(("dom", "loop"), None),
            P(("dom", "loop"), None),
            P(),
            P(("dom", "loop"), None, None),
            P(("dom", "loop"), None),
            P(("dom", "loop"), None),
            P(("dom", "loop")),
        ),
        out_specs=(P(("dom", "loop"), None), P()),
        check_vma=False,
    )
```
